32 devices in a mesh: grp: 2 (over y), row: 4 (over z), head: 2 (over x), rep: 2 (over core).
Axes of the slice: x: 2, y: 2, z: 4, core: 2. Of those that a mesh axis runs over, the one named last changes fastest.
Arguments:
- queries: float32 [2048, 8192], P(('grp', 'row', 'rep'), 'head'), parts along dimension 0
- key_max: float32 [4096, 1024], P(('grp', 'row', 'rep'), 'head'), parts along dimension 0
- key_min: float32 [4096, 1024], P(('grp', 'row', 'rep'), 'head'), parts along dimension 0, as said below
- limits: int32 [2048], P(('grp', 'row', 'rep')), parts along dimension 0, may hold values from 0 to 2047, as said below
Outputs:
- page_mass: float32 [2048, 2048], P(('grp', 'row', 'rep'), 'head'), parts along dimension 0
The draws below stay inside these ranges and needn't reach their ends.
There are 2 independent parts, one for each index of `grp`. The reference program is written for one: setup_inputs(seed, part) draws one part's arguments, and reference() takes and returns one part's arrays. A program takes and returns all parts, laid end to end along the dimension named above; each array names one. Nothing has to cross between parts.
Inputs may be any that keep to these rules, and one draw needn't show every extreme that they name: key_min <= key_max in every entry. Rows of the i-th aligned block of 128 rows have limits within the i-th block of 256 pages, not falling within a block; the first block's first row has the first page and the last block's last row the last page.
All inputs are finite; a program needn't handle non-finite values.
Results may differ from the reference program's by a relative error of at most 0.00013.
Values sent between devices are 32-bit elements; how exact they have to be, the bound alone decides.
No kernel may reach another device: no remote copies, remote signals or barrier semaphores. Data moves between devices by JAX's collectives and lax.ppermute only.
A program may use at most 64 MiB of HBM per device.

```python
import math
import jax
import jax.numpy as jnp
from jax import lax

H = 64
KVH = 8
DH = 128
ROW_DEV = 128
PAGE_DEV = 256
ROWS = 1024
PAGES = 2048


def bound_sheets(key):
    center = jax.random.normal(jax.random.fold_in(key, 101), (PAGES, KVH * DH), jnp.float32)
    center = jnp.clip(center, -6.0, 6.0)
    upper_gap = jnp.exp(jax.random.uniform(jax.random.fold_in(key, 102), (PAGES, KVH * DH), jnp.float32, math.log(0.2), 0.0))
    lower_gap = jnp.exp(jax.random.uniform(jax.random.fold_in(key, 103), (PAGES, KVH * DH), jnp.float32, math.log(0.2), 0.0))
    return (center + upper_gap, center - lower_gap)


def draw_key_max(key, part):
    return bound_sheets(key)[0]


def draw_key_min(key, part):
    return bound_sheets(key)[1]


def draw_queries(key, part):
    samples = jnp.clip(jax.random.normal(key, (ROWS, H * DH), jnp.float32), -6.0, 6.0)
    return samples


def draw_limits(key, part):
    block_count = ROWS // ROW_DEV
    offsets = jax.random.randint(key, (ROWS,), 0, PAGE_DEV, dtype=jnp.int32)
    offsets = offsets.at[0].set(0).at[ROWS - 1].set(PAGE_DEV - 1)
    offsets = jnp.sort(offsets.reshape(block_count, ROW_DEV), axis=1)
    block_start = (jnp.arange(block_count, dtype=jnp.int32) * PAGE_DEV)[:, None]
    return (offsets + block_start).reshape(ROWS).astype(jnp.int32)


def setup_inputs(seed: int = 0, part: int = 0) -> dict:
    keys = jax.random.split(jax.random.key(seed), 5)
    own_keys = jax.random.split(jax.random.fold_in(keys[4], part), 5)
    return {
        "queries": draw_queries(jax.random.fold_in(jax.random.fold_in(keys[4], part), 71), part),
        "key_max": draw_key_max(jax.random.fold_in(jax.random.fold_in(keys[4], part), 71), part),
        "key_min": draw_key_min(jax.random.fold_in(jax.random.fold_in(keys[4], part), 71), part),
        "limits": draw_limits(jax.random.fold_in(jax.random.fold_in(keys[4], part), 71), part),
    }


def reference(queries, key_max, key_min, limits):
    score_scale = 1.0 / math.sqrt(DH)
    group_size = H // KVH
    head_rows = queries.reshape(ROWS, H, DH).transpose(1, 0, 2)
    positive = jnp.maximum(head_rows, 0.0)
    negative = jnp.minimum(head_rows, 0.0)
    upper_keys = jnp.repeat(key_max.reshape(PAGES, KVH, DH).transpose(1, 0, 2), group_size, axis=0)
    lower_keys = jnp.repeat(key_min.reshape(PAGES, KVH, DH).transpose(1, 0, 2), group_size, axis=0)
    page_ids = jnp.arange(PAGES, dtype=jnp.int32)
    visible = page_ids[None, :] <= limits.astype(jnp.int32)[:, None]

    def head_step(accumulated, pieces):
        pos_rows, neg_rows, upper, lower = pieces
        raw_scores = jnp.dot(pos_rows, upper.T, precision=lax.Precision.HIGHEST)
        raw_scores = raw_scores + jnp.dot(neg_rows, lower.T, precision=lax.Precision.HIGHEST)
        masked = jnp.where(visible, raw_scores * score_scale, -1e+30)
        row_top = lax.optimization_barrier(jnp.max(masked, axis=1, keepdims=True))
        weights = jnp.exp(masked - row_top)
        row_total = lax.optimization_barrier(jnp.sum(weights, axis=1, keepdims=True))
        return (accumulated + weights / row_total, None)
    start = jnp.zeros((ROWS, PAGES), jnp.float32)
    accumulated, unused = lax.scan(head_step, start, (positive, negative, upper_keys, lower_keys))
    return accumulated
```

```python
import functools
import math

import jax
import jax.numpy as jnp
from jax import lax
from jax.experimental import pallas as pl
from jax.experimental.pallas import tpu as pltpu
from jax.sharding import PartitionSpec as P

DH = 128
CHUNK = 256
ROW_STRIP = 8


def _split(x):
    hi = x.astype(jnp.bfloat16)
    lo = (x - hi.astype(jnp.float32)).astype(jnp.bfloat16)
    return hi, lo


def _mass_kernel(nb_ref, q_ref, k_ref, lim_ref, out_ref, khi_ref, klo_ref, s_ref,
                 *, group_size, chunk_count, score_scale):
    h = pl.program_id(0)
    nb = nb_ref[0]
    row_count, page_count = s_ref.shape

    @pl.when(h == 0)
    def _():
        out_ref[...] = jnp.zeros_like(out_ref)

    @pl.when(h % group_size == 0)
    def _():
        for c in range(chunk_count):
            @pl.when(c < nb)
            def _():
                kc = k_ref[c * CHUNK:(c + 1) * CHUNK, :].T
                hi, lo = _split(kc)
                khi_ref[:, c * CHUNK:(c + 1) * CHUNK] = hi
                klo_ref[:, c * CHUNK:(c + 1) * CHUNK] = lo

    q = q_ref[...]
    x = jnp.concatenate([jnp.maximum(q, 0.0), jnp.minimum(q, 0.0)], axis=1) * score_scale
    xhi, xlo = _split(x)

    for c in range(chunk_count):
        @pl.when(c < nb)
        def _():
            khi = khi_ref[:, c * CHUNK:(c + 1) * CHUNK]
            klo = klo_ref[:, c * CHUNK:(c + 1) * CHUNK]
            s = jnp.dot(xhi, khi, preferred_element_type=jnp.float32)
            s = s + jnp.dot(xhi, klo, preferred_element_type=jnp.float32)
            s = s + jnp.dot(xlo, khi, preferred_element_type=jnp.float32)
            s_ref[:, c * CHUNK:(c + 1) * CHUNK] = s

    def strip(i, carry):
        r0 = pl.multiple_of(i * ROW_STRIP, ROW_STRIP)
        sv = s_ref[pl.ds(r0, ROW_STRIP), :]
        lim = lim_ref[pl.ds(r0, ROW_STRIP), :]
        pages = lax.broadcasted_iota(jnp.int32, sv.shape, 1)
        sm = jnp.where(pages <= lim, sv, -1e30)
        top = jnp.max(sm, axis=1, keepdims=True)
        e = jnp.exp(sm - top)
        total = jnp.sum(e, axis=1, keepdims=True)
        out_ref[pl.ds(r0, ROW_STRIP), :] += e * (1.0 / total)
        return carry

    lax.fori_loop(0, row_count // ROW_STRIP, strip, 0)


def page_mass_local(queries, keys, limits):
    row_count = queries.shape[0]
    head_count = queries.shape[1] // DH
    page_count = keys.shape[0]
    kv_count = keys.shape[1] // (2 * DH)
    group_size = head_count // kv_count
    chunk_count = page_count // CHUNK
    nb = (jnp.max(limits) // CHUNK + 1).astype(jnp.int32).reshape(1)
    kernel = functools.partial(
        _mass_kernel, group_size=group_size, chunk_count=chunk_count,
        score_scale=1.0 / math.sqrt(DH))
    grid_spec = pltpu.PrefetchScalarGridSpec(
        num_scalar_prefetch=1,
        grid=(head_count,),
        in_specs=[
            pl.BlockSpec((row_count, DH), lambda h, nb: (0, h)),
            pl.BlockSpec((page_count, 2 * DH), lambda h, nb: (0, h // group_size)),
            pl.BlockSpec((row_count, 1), lambda h, nb: (0, 0)),
        ],
        out_specs=pl.BlockSpec((row_count, page_count), lambda h, nb: (0, 0)),
        scratch_shapes=[
            pltpu.VMEM((2 * DH, page_count), jnp.bfloat16),
            pltpu.VMEM((2 * DH, page_count), jnp.bfloat16),
            pltpu.VMEM((row_count, page_count), jnp.float32),
        ],
    )
    return pl.pallas_call(
        kernel,
        grid_spec=grid_spec,
        out_shape=jax.ShapeDtypeStruct((row_count, page_count), jnp.float32),
        compiler_params=pltpu.CompilerParams(dimension_semantics=("arbitrary",)),
    )(nb, queries, keys, limits.reshape(row_count, 1))


def per_device(queries, key_max, key_min, limits):
    local_pages = key_max.shape[0]
    kv_count = key_max.shape[1] // DH
    bounds = jnp.stack(
        (key_max.reshape(local_pages, kv_count, DH), key_min.reshape(local_pages, kv_count, DH)),
        axis=2,
    ).reshape(local_pages, kv_count * 2 * DH)
    keys = lax.all_gather(bounds, ("row", "rep"), axis=0, tiled=True)
    accumulated = page_mass_local(queries, keys, limits)
    return lax.psum_scatter(accumulated, "head", scatter_dimension=1, tiled=True)


def solution(mesh):
    placed = (
        P(("grp", "row", "rep"), "head"),
        P(("grp", "row", "rep"), "head"),
        P(("grp", "row", "rep"), "head"),
        P(("grp", "row", "rep")),
    )
    return jax.shard_map(
        per_device,
        mesh=mesh,
        in_specs=placed,
        out_specs=P(("grp", "row", "rep"), "head"),
        check_vma=False,
    )
```

```python
import functools
import math

import jax
import jax.numpy as jnp
from jax import lax
from jax.experimental import pallas as pl
from jax.experimental.pallas import tpu as pltpu
from jax.sharding import PartitionSpec as P

DH = 128
CHUNK = 256


def _split(x):
    hi = x.astype(jnp.bfloat16)
    lo = (x - hi.astype(jnp.float32)).astype(jnp.bfloat16)
    return hi, lo


def _mass_kernel(nb_ref, q_ref, k_ref, lim_ref, out_ref, khi_ref, klo_ref, s_ref, acc_ref,
                 *, group_size, chunk_count, score_scale):
    h = pl.program_id(0)
    nb = nb_ref[0]
    row_count = q_ref.shape[0]

    @pl.when(h == 0)
    def _():
        acc_ref[...] = jnp.zeros_like(acc_ref)

    @pl.when(h % group_size == 0)
    def _():
        for c in range(chunk_count):
            @pl.when(c < nb)
            def _():
                hi, lo = _split(k_ref[c * CHUNK:(c + 1) * CHUNK, :])
                khi_ref[c * CHUNK:(c + 1) * CHUNK, :] = hi
                klo_ref[c * CHUNK:(c + 1) * CHUNK, :] = lo

    q = q_ref[...]
    x = jnp.concatenate([jnp.maximum(q, 0.0), jnp.minimum(q, 0.0)], axis=1) * score_scale
    xhi, xlo = _split(x.T)
    lim = lim_ref[...]
    page_in_chunk = lax.broadcasted_iota(jnp.int32, (CHUNK, row_count), 0)

    def vreg_fold(v, op):
        return op(v.reshape(CHUNK // 8, 8, row_count), axis=0)

    top = jnp.full((8, row_count), -jnp.inf, jnp.float32)
    for c in range(chunk_count):
        def pass_scores(top, c=c):
            khi = khi_ref[c * CHUNK:(c + 1) * CHUNK, :]
            klo = klo_ref[c * CHUNK:(c + 1) * CHUNK, :]
            s = jnp.dot(khi, xhi, preferred_element_type=jnp.float32)
            s = s + jnp.dot(khi, xlo, preferred_element_type=jnp.float32)
            s = s + jnp.dot(klo, xhi, preferred_element_type=jnp.float32)
            s = jnp.where(page_in_chunk + c * CHUNK <= lim, s, -1e30)
            s_ref[c * CHUNK:(c + 1) * CHUNK, :] = s
            return jnp.maximum(top, vreg_fold(s, jnp.max))
        top = lax.cond(c < nb, pass_scores, lambda t: t, top)
    top = jnp.max(top, axis=0, keepdims=True)

    total = jnp.zeros((8, row_count), jnp.float32)
    for c in range(chunk_count):
        def pass_exp(total, c=c):
            e = jnp.exp(s_ref[c * CHUNK:(c + 1) * CHUNK, :] - top)
            s_ref[c * CHUNK:(c + 1) * CHUNK, :] = e
            return total + vreg_fold(e, jnp.sum)
        total = lax.cond(c < nb, pass_exp, lambda t: t, total)
    inv = 1.0 / jnp.sum(total, axis=0, keepdims=True)

    for c in range(chunk_count):
        @pl.when(c < nb)
        def _():
            acc_ref[c * CHUNK:(c + 1) * CHUNK, :] += s_ref[c * CHUNK:(c + 1) * CHUNK, :] * inv

    @pl.when(h == pl.num_programs(0) - 1)
    def _():
        for c in range(chunk_count):
            out_ref[:, c * CHUNK:(c + 1) * CHUNK] = acc_ref[c * CHUNK:(c + 1) * CHUNK, :].T


def page_mass_local(queries, keys, limits):
    row_count = queries.shape[0]
    head_count = queries.shape[1] // DH
    page_count = keys.shape[0]
    kv_count = keys.shape[1] // (2 * DH)
    group_size = head_count // kv_count
    chunk_count = page_count // CHUNK
    nb = (jnp.max(limits) // CHUNK + 1).astype(jnp.int32).reshape(1)
    kernel = functools.partial(
        _mass_kernel, group_size=group_size, chunk_count=chunk_count,
        score_scale=1.0 / math.sqrt(DH))
    grid_spec = pltpu.PrefetchScalarGridSpec(
        num_scalar_prefetch=1,
        grid=(head_count,),
        in_specs=[
            pl.BlockSpec((row_count, DH), lambda h, nb: (0, h)),
            pl.BlockSpec((page_count, 2 * DH), lambda h, nb: (0, h // group_size)),
            pl.BlockSpec((1, row_count), lambda h, nb: (0, 0)),
        ],
        out_specs=pl.BlockSpec((row_count, page_count), lambda h, nb: (0, 0)),
        scratch_shapes=[
            pltpu.VMEM((page_count, 2 * DH), jnp.bfloat16),
            pltpu.VMEM((page_count, 2 * DH), jnp.bfloat16),
            pltpu.VMEM((page_count, row_count), jnp.float32),
            pltpu.VMEM((page_count, row_count), jnp.float32),
        ],
    )
    return pl.pallas_call(
        kernel,
        grid_spec=grid_spec,
        out_shape=jax.ShapeDtypeStruct((row_count, page_count), jnp.float32),
        compiler_params=pltpu.CompilerParams(dimension_semantics=("arbitrary",)),
    )(nb, queries, keys, limits.reshape(1, row_count))


def per_device(queries, key_max, key_min, limits):
    local_pages = key_max.shape[0]
    kv_count = key_max.shape[1] // DH
    bounds = jnp.stack(
        (key_max.reshape(local_pages, kv_count, DH), key_min.reshape(local_pages, kv_count, DH)),
        axis=2,
    ).reshape(local_pages, kv_count * 2 * DH)
    keys = lax.all_gather(bounds, ("row", "rep"), axis=0, tiled=True)
    accumulated = page_mass_local(queries, keys, limits)
    return lax.psum_scatter(accumulated, "head", scatter_dimension=1, tiled=True)


def solution(mesh):
    placed = (
        P(("grp", "row", "rep"), "head"),
        P(("grp", "row", "rep"), "head"),
        P(("grp", "row", "rep"), "head"),
        P(("grp", "row", "rep")),
    )
    return jax.shard_map(
        per_device,
        mesh=mesh,
        in_specs=placed,
        out_specs=P(("grp", "row", "rep"), "head"),
        check_vma=False,
    )
```

```python
import functools
import math

import jax
import jax.numpy as jnp
from jax import lax
from jax.experimental import pallas as pl
from jax.experimental.pallas import tpu as pltpu
from jax.sharding import PartitionSpec as P

DH = 128
CHUNK = 256


def _split(x):
    hi = x.astype(jnp.bfloat16)
    lo = (x - hi.astype(jnp.float32)).astype(jnp.bfloat16)
    return hi, lo


def _mass_kernel(nb_ref, q_ref, k_ref, lim_ref, out_ref, kcat_ref, s_ref, acc_ref,
                 *, pairs_per_group, chunk_count, score_scale):
    hp = pl.program_id(0)
    nb = nb_ref[0]
    row_count = q_ref.shape[0] // 1
    lanes = 2 * row_count

    @pl.when(hp == 0)
    def _():
        acc_ref[...] = jnp.zeros_like(acc_ref)

    @pl.when(hp % pairs_per_group == 0)
    def _():
        for c in range(chunk_count):
            @pl.when(c < nb)
            def _():
                hi, lo = _split(k_ref[c * CHUNK:(c + 1) * CHUNK, :])
                kcat_ref[c * CHUNK:(c + 1) * CHUNK, :] = jnp.concatenate([hi, hi, lo], axis=1)

    q = q_ref[...]
    xs = []
    for j in range(2):
        qj = q[:, j * DH:(j + 1) * DH]
        xs.append(jnp.concatenate([jnp.maximum(qj, 0.0), jnp.minimum(qj, 0.0)], axis=1).T)
    w = jnp.concatenate(xs, axis=1) * score_scale
    whi, wlo = _split(w)
    wcat = jnp.concatenate([whi, wlo, whi], axis=0)
    lim = lim_ref[...]
    lim2 = jnp.concatenate([lim, lim], axis=1)
    page_in_chunk = lax.broadcasted_iota(jnp.int32, (CHUNK, lanes), 0)

    def vreg_fold(v, op):
        return op(v.reshape(CHUNK // 8, 8, lanes), axis=0)

    top = jnp.full((8, lanes), -jnp.inf, jnp.float32)
    for c in range(chunk_count):
        def pass_scores(top, c=c):
            s = jnp.dot(kcat_ref[c * CHUNK:(c + 1) * CHUNK, :], wcat,
                        preferred_element_type=jnp.float32)
            s = jnp.where(page_in_chunk + c * CHUNK <= lim2, s, -1e30)
            s_ref[c * CHUNK:(c + 1) * CHUNK, :] = s
            return jnp.maximum(top, vreg_fold(s, jnp.max))
        top = lax.cond(c < nb, pass_scores, lambda t: t, top)
    top = jnp.max(top, axis=0, keepdims=True)

    total = jnp.zeros((8, lanes), jnp.float32)
    for c in range(chunk_count):
        def pass_exp(total, c=c):
            e = jnp.exp(s_ref[c * CHUNK:(c + 1) * CHUNK, :] - top)
            s_ref[c * CHUNK:(c + 1) * CHUNK, :] = e
            return total + vreg_fold(e, jnp.sum)
        total = lax.cond(c < nb, pass_exp, lambda t: t, total)
    inv = 1.0 / jnp.sum(total, axis=0, keepdims=True)
    inv_a = inv[:, :row_count]
    inv_b = inv[:, row_count:]

    for c in range(chunk_count):
        @pl.when(c < nb)
        def _():
            e = s_ref[c * CHUNK:(c + 1) * CHUNK, :]
            acc_ref[c * CHUNK:(c + 1) * CHUNK, :] += (
                e[:, :row_count] * inv_a + e[:, row_count:] * inv_b)

    @pl.when(hp == pl.num_programs(0) - 1)
    def _():
        for c in range(chunk_count):
            out_ref[:, c * CHUNK:(c + 1) * CHUNK] = acc_ref[c * CHUNK:(c + 1) * CHUNK, :].T


def page_mass_local(queries, keys, limits):
    row_count = queries.shape[0]
    head_count = queries.shape[1] // DH
    page_count = keys.shape[0]
    kv_count = keys.shape[1] // (2 * DH)
    pairs_per_group = head_count // kv_count // 2
    chunk_count = page_count // CHUNK
    nb = (jnp.max(limits) // CHUNK + 1).astype(jnp.int32).reshape(1)
    kernel = functools.partial(
        _mass_kernel, pairs_per_group=pairs_per_group, chunk_count=chunk_count,
        score_scale=1.0 / math.sqrt(DH))
    grid_spec = pltpu.PrefetchScalarGridSpec(
        num_scalar_prefetch=1,
        grid=(head_count // 2,),
        in_specs=[
            pl.BlockSpec((row_count, 2 * DH), lambda hp, nb: (0, hp)),
            pl.BlockSpec((page_count, 2 * DH), lambda hp, nb: (0, hp // pairs_per_group)),
            pl.BlockSpec((1, row_count), lambda hp, nb: (0, 0)),
        ],
        out_specs=pl.BlockSpec((row_count, page_count), lambda hp, nb: (0, 0)),
        scratch_shapes=[
            pltpu.VMEM((page_count, 6 * DH), jnp.bfloat16),
            pltpu.VMEM((page_count, 2 * row_count), jnp.float32),
            pltpu.VMEM((page_count, row_count), jnp.float32),
        ],
    )
    return pl.pallas_call(
        kernel,
        grid_spec=grid_spec,
        out_shape=jax.ShapeDtypeStruct((row_count, page_count), jnp.float32),
        compiler_params=pltpu.CompilerParams(dimension_semantics=("arbitrary",)),
    )(nb, queries, keys, limits.reshape(1, row_count))


def per_device(queries, key_max, key_min, limits):
    local_pages = key_max.shape[0]
    kv_count = key_max.shape[1] // DH
    bounds = jnp.stack(
        (key_max.reshape(local_pages, kv_count, DH), key_min.reshape(local_pages, kv_count, DH)),
        axis=2,
    ).reshape(local_pages, kv_count * 2 * DH)
    keys = lax.all_gather(bounds, ("row", "rep"), axis=0, tiled=True)
    accumulated = page_mass_local(queries, keys, limits)
    return lax.psum_scatter(accumulated, "head", scatter_dimension=1, tiled=True)


def solution(mesh):
    placed = (
        P(("grp", "row", "rep"), "head"),
        P(("grp", "row", "rep"), "head"),
        P(("grp", "row", "rep"), "head"),
        P(("grp", "row", "rep")),
    )
    return jax.shard_map(
        per_device,
        mesh=mesh,
        in_specs=placed,
        out_specs=P(("grp", "row", "rep"), "head"),
        check_vma=False,
    )
```

```python
import functools
import math

import jax
import jax.numpy as jnp
from jax import lax
from jax.experimental import pallas as pl
from jax.experimental.pallas import tpu as pltpu
from jax.sharding import PartitionSpec as P

DH = 128
CHUNK = 256


def _split(x):
    hi = x.astype(jnp.bfloat16)
    lo = (x - hi.astype(jnp.float32)).astype(jnp.bfloat16)
    return hi, lo


def _mass_kernel(nb_ref, q_ref, k_ref, lim_ref, *refs, chunk_count, score_scale, first, last):
    if first:
        out_ref, kcat_ref, s_ref, acc_ref = refs
    else:
        acc_in_ref, out_ref, kcat_ref, s_ref, acc_ref = refs
    hp = pl.program_id(0)
    nb = nb_ref[0]
    row_count = q_ref.shape[0]
    lanes = 2 * row_count

    @pl.when(hp == 0)
    def _():
        if first:
            acc_ref[...] = jnp.zeros_like(acc_ref)
        else:
            acc_ref[...] = acc_in_ref[...]
        for c in range(chunk_count):
            @pl.when(c < nb)
            def _():
                hi, lo = _split(k_ref[c * CHUNK:(c + 1) * CHUNK, :])
                kcat_ref[c * CHUNK:(c + 1) * CHUNK, :] = jnp.concatenate([hi, hi, lo], axis=1)

    q = q_ref[...]
    xs = []
    for j in range(2):
        qj = q[:, j * DH:(j + 1) * DH]
        xs.append(jnp.concatenate([jnp.maximum(qj, 0.0), jnp.minimum(qj, 0.0)], axis=1).T)
    w = jnp.concatenate(xs, axis=1) * score_scale
    whi, wlo = _split(w)
    wcat = jnp.concatenate([whi, wlo, whi], axis=0)
    lim = lim_ref[...]
    lim2 = jnp.concatenate([lim, lim], axis=1)
    page_in_chunk = lax.broadcasted_iota(jnp.int32, (CHUNK, lanes), 0)

    def vreg_fold(v, op):
        return op(v.reshape(CHUNK // 8, 8, lanes), axis=0)

    top = jnp.full((8, lanes), -jnp.inf, jnp.float32)
    for c in range(chunk_count):
        def pass_scores(top, c=c):
            s = jnp.dot(kcat_ref[c * CHUNK:(c + 1) * CHUNK, :], wcat,
                        preferred_element_type=jnp.float32)
            s = jnp.where(page_in_chunk + c * CHUNK <= lim2, s, -1e30)
            s_ref[c * CHUNK:(c + 1) * CHUNK, :] = s
            return jnp.maximum(top, vreg_fold(s, jnp.max))
        top = lax.cond(c < nb, pass_scores, lambda t: t, top)
    top = jnp.max(top, axis=0, keepdims=True)

    total = jnp.zeros((8, lanes), jnp.float32)
    for c in range(chunk_count):
        def pass_exp(total, c=c):
            e = jnp.exp(s_ref[c * CHUNK:(c + 1) * CHUNK, :] - top)
            s_ref[c * CHUNK:(c + 1) * CHUNK, :] = e
            return total + vreg_fold(e, jnp.sum)
        total = lax.cond(c < nb, pass_exp, lambda t: t, total)
    inv = 1.0 / jnp.sum(total, axis=0, keepdims=True)
    inv_a = inv[:, :row_count]
    inv_b = inv[:, row_count:]

    for c in range(chunk_count):
        @pl.when(c < nb)
        def _():
            e = s_ref[c * CHUNK:(c + 1) * CHUNK, :]
            acc_ref[c * CHUNK:(c + 1) * CHUNK, :] += (
                e[:, :row_count] * inv_a + e[:, row_count:] * inv_b)

    @pl.when(hp == pl.num_programs(0) - 1)
    def _():
        for c in range(chunk_count):
            if last:
                out_ref[:, c * CHUNK:(c + 1) * CHUNK] = acc_ref[c * CHUNK:(c + 1) * CHUNK, :].T
            else:
                out_ref[c * CHUNK:(c + 1) * CHUNK, :] = acc_ref[c * CHUNK:(c + 1) * CHUNK, :]


def page_mass_group(nb, queries, keys, limits, acc, last):
    row_count = queries.shape[0]
    pair_count = queries.shape[1] // (2 * DH)
    page_count = keys.shape[0]
    chunk_count = page_count // CHUNK
    first = acc is None
    kernel = functools.partial(
        _mass_kernel, chunk_count=chunk_count, score_scale=1.0 / math.sqrt(DH),
        first=first, last=last)
    in_specs = [
        pl.BlockSpec((row_count, 2 * DH), lambda hp, nb: (0, hp)),
        pl.BlockSpec((page_count, 2 * DH), lambda hp, nb: (0, 0)),
        pl.BlockSpec((1, row_count), lambda hp, nb: (0, 0)),
    ]
    operands = [nb, queries, keys, limits.reshape(1, row_count)]
    if not first:
        in_specs.append(pl.BlockSpec((page_count, row_count), lambda hp, nb: (0, 0)))
        operands.append(acc)
    if last:
        out_shape = (row_count, page_count)
    else:
        out_shape = (page_count, row_count)
    aliases = {4: 0} if (not first and not last) else {}
    grid_spec = pltpu.PrefetchScalarGridSpec(
        num_scalar_prefetch=1,
        grid=(pair_count,),
        in_specs=in_specs,
        out_specs=pl.BlockSpec(out_shape, lambda hp, nb: (0, 0)),
        scratch_shapes=[
            pltpu.VMEM((page_count, 6 * DH), jnp.bfloat16),
            pltpu.VMEM((page_count, 2 * row_count), jnp.float32),
            pltpu.VMEM((page_count, row_count), jnp.float32),
        ],
    )
    return pl.pallas_call(
        kernel,
        grid_spec=grid_spec,
        out_shape=jax.ShapeDtypeStruct(out_shape, jnp.float32),
        input_output_aliases=aliases,
        compiler_params=pltpu.CompilerParams(dimension_semantics=("arbitrary",)),
    )(*operands)


def per_device(queries, key_max, key_min, limits):
    local_pages = key_max.shape[0]
    kv_count = key_max.shape[1] // DH
    group_cols = queries.shape[1] // kv_count
    nb = (jnp.max(limits) // CHUNK + 1).astype(jnp.int32).reshape(1)
    acc = None
    for kv in range(kv_count):
        bounds = jnp.concatenate(
            (key_max[:, kv * DH:(kv + 1) * DH], key_min[:, kv * DH:(kv + 1) * DH]), axis=1)
        keys = lax.all_gather(bounds, ("row", "rep"), axis=0, tiled=True)
        acc = page_mass_group(
            nb, queries[:, kv * group_cols:(kv + 1) * group_cols], keys, limits, acc,
            last=kv == kv_count - 1)
    return lax.psum_scatter(acc, "head", scatter_dimension=1, tiled=True)


def solution(mesh):
    placed = (
        P(("grp", "row", "rep"), "head"),
        P(("grp", "row", "rep"), "head"),
        P(("grp", "row", "rep"), "head"),
        P(("grp", "row", "rep")),
    )
    return jax.shard_map(
        per_device,
        mesh=mesh,
        in_specs=placed,
        out_specs=P(("grp", "row", "rep"), "head"),
        check_vma=False,
    )
```

```python
import functools
import math

import jax
import jax.numpy as jnp
from jax import lax
from jax.experimental import pallas as pl
from jax.experimental.pallas import tpu as pltpu
from jax.sharding import PartitionSpec as P

DH = 128
CHUNK = 256
GATHERS = 2


def _split(x):
    hi = x.astype(jnp.bfloat16)
    lo = (x - hi.astype(jnp.float32)).astype(jnp.bfloat16)
    return hi, lo


def _mass_kernel(nb_ref, q_ref, k_ref, lim_ref, *refs, chunk_count, score_scale, first, last,
                 pairs_per_kv):
    if first:
        out_ref, kcat_ref, s_ref, acc_ref = refs
    else:
        acc_in_ref, out_ref, kcat_ref, s_ref, acc_ref = refs
    hp = pl.program_id(0)
    nb = nb_ref[0]
    row_count = q_ref.shape[0]
    lanes = 2 * row_count

    @pl.when(hp == 0)
    def _():
        if first:
            acc_ref[...] = jnp.zeros_like(acc_ref)
        else:
            acc_ref[...] = acc_in_ref[...]

    @pl.when(hp % pairs_per_kv == 0)
    def _():
        for c in range(chunk_count):
            @pl.when(c < nb)
            def _():
                hi, lo = _split(k_ref[c * CHUNK:(c + 1) * CHUNK, :])
                kcat_ref[c * CHUNK:(c + 1) * CHUNK, :] = jnp.concatenate([hi, hi, lo], axis=1)

    q = q_ref[...]
    xs = []
    for j in range(2):
        qj = q[:, j * DH:(j + 1) * DH]
        xs.append(jnp.concatenate([jnp.maximum(qj, 0.0), jnp.minimum(qj, 0.0)], axis=1).T)
    w = jnp.concatenate(xs, axis=1) * score_scale
    whi, wlo = _split(w)
    wcat = jnp.concatenate([whi, wlo, whi], axis=0)
    lim = lim_ref[...]
    lim2 = jnp.concatenate([lim, lim], axis=1)
    page_in_chunk = lax.broadcasted_iota(jnp.int32, (CHUNK, lanes), 0)

    def vreg_fold(v, op):
        return op(v.reshape(CHUNK // 8, 8, lanes), axis=0)

    top = jnp.full((8, lanes), -jnp.inf, jnp.float32)
    for c in range(chunk_count):
        def pass_scores(top, c=c):
            s = jnp.dot(kcat_ref[c * CHUNK:(c + 1) * CHUNK, :], wcat,
                        preferred_element_type=jnp.float32)
            s = jnp.where(page_in_chunk + c * CHUNK <= lim2, s, -1e30)
            s_ref[c * CHUNK:(c + 1) * CHUNK, :] = s
            return jnp.maximum(top, vreg_fold(s, jnp.max))
        top = lax.cond(c < nb, pass_scores, lambda t: t, top)
    top = jnp.max(top, axis=0, keepdims=True)

    total = jnp.zeros((8, lanes), jnp.float32)
    for c in range(chunk_count):
        def pass_exp(total, c=c):
            e = jnp.exp(s_ref[c * CHUNK:(c + 1) * CHUNK, :] - top)
            s_ref[c * CHUNK:(c + 1) * CHUNK, :] = e
            return total + vreg_fold(e, jnp.sum)
        total = lax.cond(c < nb, pass_exp, lambda t: t, total)
    inv = 1.0 / jnp.sum(total, axis=0, keepdims=True)
    inv_a = inv[:, :row_count]
    inv_b = inv[:, row_count:]

    for c in range(chunk_count):
        @pl.when(c < nb)
        def _():
            e = s_ref[c * CHUNK:(c + 1) * CHUNK, :]
            acc_ref[c * CHUNK:(c + 1) * CHUNK, :] += (
                e[:, :row_count] * inv_a + e[:, row_count:] * inv_b)

    @pl.when(hp == pl.num_programs(0) - 1)
    def _():
        for c in range(chunk_count):
            if last:
                out_ref[:, c * CHUNK:(c + 1) * CHUNK] = acc_ref[c * CHUNK:(c + 1) * CHUNK, :].T
            else:
                out_ref[c * CHUNK:(c + 1) * CHUNK, :] = acc_ref[c * CHUNK:(c + 1) * CHUNK, :]


def page_mass_group(nb, queries, keys, limits, acc, last):
    row_count = queries.shape[0]
    pair_count = queries.shape[1] // (2 * DH)
    pairs_per_kv = pair_count // (keys.shape[1] // (2 * DH))
    page_count = keys.shape[0]
    chunk_count = page_count // CHUNK
    first = acc is None
    kernel = functools.partial(
        _mass_kernel, chunk_count=chunk_count, score_scale=1.0 / math.sqrt(DH),
        first=first, last=last, pairs_per_kv=pairs_per_kv)
    in_specs = [
        pl.BlockSpec((row_count, 2 * DH), lambda hp, nb: (0, hp)),
        pl.BlockSpec((page_count, 2 * DH), lambda hp, nb: (0, hp // pairs_per_kv)),
        pl.BlockSpec((1, row_count), lambda hp, nb: (0, 0)),
    ]
    operands = [nb, queries, keys, limits.reshape(1, row_count)]
    if not first:
        in_specs.append(pl.BlockSpec((page_count, row_count), lambda hp, nb: (0, 0)))
        operands.append(acc)
    if last:
        out_shape = (row_count, page_count)
    else:
        out_shape = (page_count, row_count)
    aliases = {4: 0} if (not first and not last) else {}
    grid_spec = pltpu.PrefetchScalarGridSpec(
        num_scalar_prefetch=1,
        grid=(pair_count,),
        in_specs=in_specs,
        out_specs=pl.BlockSpec(out_shape, lambda hp, nb: (0, 0)),
        scratch_shapes=[
            pltpu.VMEM((page_count, 6 * DH), jnp.bfloat16),
            pltpu.VMEM((page_count, 2 * row_count), jnp.float32),
            pltpu.VMEM((page_count, row_count), jnp.float32),
        ],
    )
    return pl.pallas_call(
        kernel,
        grid_spec=grid_spec,
        out_shape=jax.ShapeDtypeStruct(out_shape, jnp.float32),
        input_output_aliases=aliases,
        compiler_params=pltpu.CompilerParams(dimension_semantics=("arbitrary",)),
    )(*operands)


def per_device(queries, key_max, key_min, limits):
    local_pages = key_max.shape[0]
    kv_count = key_max.shape[1] // DH
    call_count = min(kv_count, GATHERS)
    kv_per_call = kv_count // call_count
    group_cols = queries.shape[1] // call_count
    nb = (jnp.max(limits) // CHUNK + 1).astype(jnp.int32).reshape(1)
    acc = None
    for g in range(call_count):
        parts = []
        for kv in range(g * kv_per_call, (g + 1) * kv_per_call):
            parts += [key_max[:, kv * DH:(kv + 1) * DH], key_min[:, kv * DH:(kv + 1) * DH]]
        keys = lax.all_gather(jnp.concatenate(parts, axis=1), ("row", "rep"), axis=0, tiled=True)
        acc = page_mass_group(
            nb, queries[:, g * group_cols:(g + 1) * group_cols], keys, limits, acc,
            last=g == call_count - 1)
    return lax.psum_scatter(acc, "head", scatter_dimension=1, tiled=True)


def solution(mesh):
    placed = (
        P(("grp", "row", "rep"), "head"),
        P(("grp", "row", "rep"), "head"),
        P(("grp", "row", "rep"), "head"),
        P(("grp", "row", "rep")),
    )
    return jax.shard_map(
        per_device,
        mesh=mesh,
        in_specs=placed,
        out_specs=P(("grp", "row", "rep"), "head"),
        check_vma=False,
    )
```

```python
import functools
import math

import jax
import jax.numpy as jnp
from jax import lax
from jax.experimental import pallas as pl
from jax.experimental.pallas import tpu as pltpu
from jax.sharding import PartitionSpec as P

DH = 128
CHUNK = 256
GATHERS = 2


def _split(x):
    hi = x.astype(jnp.bfloat16)
    lo = (x - hi.astype(jnp.float32)).astype(jnp.bfloat16)
    return hi, lo


def _mass_kernel(nb_ref, q_ref, k_ref, lim_ref, *refs, chunk_count, score_scale, first, last,
                 pairs_per_kv):
    if first:
        out_ref, kcat_ref, s_ref, acc_ref = refs
    else:
        acc_in_ref, out_ref, kcat_ref, s_ref, acc_ref = refs
    hp = pl.program_id(0)
    nb = nb_ref[0]
    row_count = q_ref.shape[0]
    lanes = 2 * row_count

    @pl.when(hp == 0)
    def _():
        if first:
            acc_ref[...] = jnp.zeros_like(acc_ref)
        else:
            acc_ref[...] = acc_in_ref[...]

    @pl.when(hp % pairs_per_kv == 0)
    def _():
        for c in range(chunk_count):
            @pl.when(c < nb)
            def _():
                hi, lo = _split(k_ref[c * CHUNK:(c + 1) * CHUNK, :])
                kcat_ref[c * CHUNK:(c + 1) * CHUNK, :] = jnp.concatenate([hi, hi, lo], axis=1)

    q = q_ref[...]
    xs = []
    for j in range(2):
        qj = q[:, j * DH:(j + 1) * DH]
        xs.append(jnp.concatenate([jnp.maximum(qj, 0.0), jnp.minimum(qj, 0.0)], axis=1).T)
    w = jnp.concatenate(xs, axis=1) * score_scale
    whi, wlo = _split(w)
    wcat = jnp.concatenate([whi, wlo, whi], axis=0)
    lim = lim_ref[...]
    lim2 = jnp.concatenate([lim, lim], axis=1)
    page_in_chunk = lax.broadcasted_iota(jnp.int32, (CHUNK, lanes), 0)

    def vreg_fold(v, op):
        return op(v.reshape(CHUNK // 8, 8, lanes), axis=0)

    top = jnp.full((8, lanes), -jnp.inf, jnp.float32)
    for c in range(chunk_count):
        def pass_scores(top, c=c):
            s = jnp.dot(kcat_ref[c * CHUNK:(c + 1) * CHUNK, :], wcat,
                        preferred_element_type=jnp.float32)
            s = jnp.where(page_in_chunk + c * CHUNK <= lim2, s, -1e30)
            s_ref[c * CHUNK:(c + 1) * CHUNK, :] = s
            return jnp.maximum(top, vreg_fold(s, jnp.max))
        top = lax.cond(c < nb, pass_scores, lambda t: t, top)
    top = jnp.max(top, axis=0, keepdims=True)

    total = jnp.zeros((8, lanes), jnp.float32)
    for c in range(chunk_count):
        def pass_exp(total, c=c):
            e = jnp.exp(s_ref[c * CHUNK:(c + 1) * CHUNK, :] - top)
            s_ref[c * CHUNK:(c + 1) * CHUNK, :] = e
            return total + vreg_fold(e, jnp.sum)
        total = lax.cond(c < nb, pass_exp, lambda t: t, total)
    inv = 1.0 / jnp.sum(total, axis=0, keepdims=True)
    inv_a = inv[:, :row_count]
    inv_b = inv[:, row_count:]

    for c in range(chunk_count):
        @pl.when(c < nb)
        def _():
            e = s_ref[c * CHUNK:(c + 1) * CHUNK, :]
            acc_ref[c * CHUNK:(c + 1) * CHUNK, :] += (
                e[:, :row_count] * inv_a + e[:, row_count:] * inv_b)

    @pl.when(hp == pl.num_programs(0) - 1)
    def _():
        for c in range(chunk_count):
            if last:
                out_ref[:, c * CHUNK:(c + 1) * CHUNK] = acc_ref[c * CHUNK:(c + 1) * CHUNK, :].T
            else:
                out_ref[c * CHUNK:(c + 1) * CHUNK, :] = acc_ref[c * CHUNK:(c + 1) * CHUNK, :]


def page_mass_group(nb, queries, keys, limits, acc, last):
    row_count = queries.shape[0]
    pair_count = queries.shape[1] // (2 * DH)
    pairs_per_kv = pair_count // (keys.shape[1] // (2 * DH))
    page_count = keys.shape[0]
    chunk_count = page_count // CHUNK
    first = acc is None
    kernel = functools.partial(
        _mass_kernel, chunk_count=chunk_count, score_scale=1.0 / math.sqrt(DH),
        first=first, last=last, pairs_per_kv=pairs_per_kv)
    in_specs = [
        pl.BlockSpec((row_count, 2 * DH), lambda hp, nb: (0, hp)),
        pl.BlockSpec((page_count, 2 * DH), lambda hp, nb: (0, hp // pairs_per_kv)),
        pl.BlockSpec((1, row_count), lambda hp, nb: (0, 0)),
    ]
    operands = [nb, queries, keys, limits.reshape(1, row_count)]
    if not first:
        in_specs.append(pl.BlockSpec((page_count, row_count), lambda hp, nb: (0, 0)))
        operands.append(acc)
    if last:
        out_shape = (row_count, page_count)
    else:
        out_shape = (page_count, row_count)
    aliases = {4: 0} if (not first and not last) else {}
    grid_spec = pltpu.PrefetchScalarGridSpec(
        num_scalar_prefetch=1,
        grid=(pair_count,),
        in_specs=in_specs,
        out_specs=pl.BlockSpec(out_shape, lambda hp, nb: (0, 0)),
        scratch_shapes=[
            pltpu.VMEM((page_count, 6 * DH), jnp.bfloat16),
            pltpu.VMEM((page_count, 2 * row_count), jnp.float32),
            pltpu.VMEM((page_count, row_count), jnp.float32),
        ],
    )
    return pl.pallas_call(
        kernel,
        grid_spec=grid_spec,
        out_shape=jax.ShapeDtypeStruct(out_shape, jnp.float32),
        input_output_aliases=aliases,
        compiler_params=pltpu.CompilerParams(dimension_semantics=("arbitrary",)),
    )(*operands)


def head_sum_scatter(acc, head_devices):
    if head_devices != 2:
        return lax.psum_scatter(acc, "head", scatter_dimension=1, tiled=True)
    half = acc.shape[1] // 2
    first_half = lax.axis_index("head") == 0
    own = jnp.where(first_half, acc[:, :half], acc[:, half:])
    other = jnp.where(first_half, acc[:, half:], acc[:, :half])
    return own + lax.ppermute(other, "head", [(0, 1), (1, 0)])


def per_device(queries, key_max, key_min, limits, head_devices):
    local_pages = key_max.shape[0]
    kv_count = key_max.shape[1] // DH
    call_count = min(kv_count, GATHERS)
    kv_per_call = kv_count // call_count
    group_cols = queries.shape[1] // call_count
    nb = (jnp.max(limits) // CHUNK + 1).astype(jnp.int32).reshape(1)
    acc = None
    for g in range(call_count):
        parts = []
        for kv in range(g * kv_per_call, (g + 1) * kv_per_call):
            parts += [key_max[:, kv * DH:(kv + 1) * DH], key_min[:, kv * DH:(kv + 1) * DH]]
        keys = lax.all_gather(jnp.concatenate(parts, axis=1), ("row", "rep"), axis=0, tiled=True)
        acc = page_mass_group(
            nb, queries[:, g * group_cols:(g + 1) * group_cols], keys, limits, acc,
            last=g == call_count - 1)
    return head_sum_scatter(acc, head_devices)


def solution(mesh):
    placed = (
        P(("grp", "row", "rep"), "head"),
        P(("grp", "row", "rep"), "head"),
        P(("grp", "row", "rep"), "head"),
        P(("grp", "row", "rep")),
    )
    return jax.shard_map(
        functools.partial(per_device, head_devices=mesh.shape["head"]),
        mesh=mesh,
        in_specs=placed,
        out_specs=P(("grp", "row", "rep"), "head"),
        check_vma=False,
    )
```

```python
import functools
import math

import jax
import jax.numpy as jnp
from jax import lax
from jax.experimental import pallas as pl
from jax.experimental.pallas import tpu as pltpu
from jax.sharding import PartitionSpec as P

DH = 128
CHUNK = 256
GATHERS = 2
MM_CHUNK = 1024


def _split(x):
    hi = x.astype(jnp.bfloat16)
    lo = (x - hi.astype(jnp.float32)).astype(jnp.bfloat16)
    return hi, lo


def _mass_kernel(nb_ref, q_ref, k_ref, lim_ref, *refs, chunk_count, score_scale, first, last,
                 pairs_per_kv):
    if first:
        out_ref, kcat_ref, s_ref, acc_ref = refs
    else:
        acc_in_ref, out_ref, kcat_ref, s_ref, acc_ref = refs
    hp = pl.program_id(0)
    nb = nb_ref[0]
    nfull = nb_ref[1]
    row_count = q_ref.shape[0]
    lanes = 2 * row_count

    @pl.when(hp == 0)
    def _():
        if first:
            acc_ref[...] = jnp.zeros_like(acc_ref)
        else:
            acc_ref[...] = acc_in_ref[...]

    @pl.when(hp % pairs_per_kv == 0)
    def _():
        for c in range(chunk_count):
            @pl.when(c < nb)
            def _():
                hi, lo = _split(k_ref[c * CHUNK:(c + 1) * CHUNK, :])
                kcat_ref[c * CHUNK:(c + 1) * CHUNK, :] = jnp.concatenate([hi, hi, lo], axis=1)

    q = q_ref[...]
    xs = []
    for j in range(2):
        qj = q[:, j * DH:(j + 1) * DH]
        xs.append(jnp.concatenate([jnp.maximum(qj, 0.0), jnp.minimum(qj, 0.0)], axis=1).T)
    w = jnp.concatenate(xs, axis=1) * score_scale
    whi, wlo = _split(w)
    wcat = jnp.concatenate([whi, wlo, whi], axis=0)
    lim = lim_ref[...]
    lim2 = jnp.concatenate([lim, lim], axis=1)
    page_in_chunk = lax.broadcasted_iota(jnp.int32, (CHUNK, lanes), 0)

    def vreg_fold(v, op):
        return op(v.reshape(CHUNK // 8, 8, lanes), axis=0)

    mm_pages = min(MM_CHUNK, chunk_count * CHUNK)
    for mc in range(chunk_count * CHUNK // mm_pages):
        @pl.when(mc * mm_pages < nb * CHUNK)
        def _():
            s_ref[mc * mm_pages:(mc + 1) * mm_pages, :] = jnp.dot(
                kcat_ref[mc * mm_pages:(mc + 1) * mm_pages, :], wcat,
                preferred_element_type=jnp.float32)

    top = jnp.full((8, lanes), -jnp.inf, jnp.float32)
    for c in range(chunk_count):
        def keep(top):
            return top

        def open_chunk(top, c=c):
            return jnp.maximum(top, vreg_fold(s_ref[c * CHUNK:(c + 1) * CHUNK, :], jnp.max))

        def masked_chunk(top, c=c):
            s = s_ref[c * CHUNK:(c + 1) * CHUNK, :]
            s = jnp.where(page_in_chunk <= lim2 - c * CHUNK, s, -1e30)
            s_ref[c * CHUNK:(c + 1) * CHUNK, :] = s
            return jnp.maximum(top, vreg_fold(s, jnp.max))

        branch = jnp.where(c < nb, jnp.where(c < nfull, 1, 2), 0)
        top = lax.switch(branch, [keep, open_chunk, masked_chunk], top)
    top = jnp.max(top, axis=0, keepdims=True)

    total = jnp.zeros((8, lanes), jnp.float32)
    for c in range(chunk_count):
        def pass_exp(total, c=c):
            e = jnp.exp(s_ref[c * CHUNK:(c + 1) * CHUNK, :] - top)
            s_ref[c * CHUNK:(c + 1) * CHUNK, :] = e
            return total + vreg_fold(e, jnp.sum)
        total = lax.cond(c < nb, pass_exp, lambda t: t, total)
    inv = 1.0 / jnp.sum(total, axis=0, keepdims=True)
    inv_a = inv[:, :row_count]
    inv_b = inv[:, row_count:]

    for c in range(chunk_count):
        @pl.when(c < nb)
        def _():
            e = s_ref[c * CHUNK:(c + 1) * CHUNK, :]
            acc_ref[c * CHUNK:(c + 1) * CHUNK, :] += (
                e[:, :row_count] * inv_a + e[:, row_count:] * inv_b)

    @pl.when(hp == pl.num_programs(0) - 1)
    def _():
        for c in range(chunk_count):
            if last:
                out_ref[:, c * CHUNK:(c + 1) * CHUNK] = acc_ref[c * CHUNK:(c + 1) * CHUNK, :].T
            else:
                out_ref[c * CHUNK:(c + 1) * CHUNK, :] = acc_ref[c * CHUNK:(c + 1) * CHUNK, :]


def page_mass_group(nb, queries, keys, limits, acc, last):
    row_count = queries.shape[0]
    pair_count = queries.shape[1] // (2 * DH)
    pairs_per_kv = pair_count // (keys.shape[1] // (2 * DH))
    page_count = keys.shape[0]
    chunk_count = page_count // CHUNK
    first = acc is None
    kernel = functools.partial(
        _mass_kernel, chunk_count=chunk_count, score_scale=1.0 / math.sqrt(DH),
        first=first, last=last, pairs_per_kv=pairs_per_kv)
    in_specs = [
        pl.BlockSpec((row_count, 2 * DH), lambda hp, nb: (0, hp)),
        pl.BlockSpec((page_count, 2 * DH), lambda hp, nb: (0, hp // pairs_per_kv)),
        pl.BlockSpec((1, row_count), lambda hp, nb: (0, 0)),
    ]
    operands = [nb, queries, keys, limits.reshape(1, row_count)]
    if not first:
        in_specs.append(pl.BlockSpec((page_count, row_count), lambda hp, nb: (0, 0)))
        operands.append(acc)
    if last:
        out_shape = (row_count, page_count)
    else:
        out_shape = (page_count, row_count)
    aliases = {4: 0} if (not first and not last) else {}
    grid_spec = pltpu.PrefetchScalarGridSpec(
        num_scalar_prefetch=1,
        grid=(pair_count,),
        in_specs=in_specs,
        out_specs=pl.BlockSpec(out_shape, lambda hp, nb: (0, 0)),
        scratch_shapes=[
            pltpu.VMEM((page_count, 6 * DH), jnp.bfloat16),
            pltpu.VMEM((page_count, 2 * row_count), jnp.float32),
            pltpu.VMEM((page_count, row_count), jnp.float32),
        ],
    )
    return pl.pallas_call(
        kernel,
        grid_spec=grid_spec,
        out_shape=jax.ShapeDtypeStruct(out_shape, jnp.float32),
        input_output_aliases=aliases,
        compiler_params=pltpu.CompilerParams(dimension_semantics=("arbitrary",)),
    )(*operands)


def head_sum_scatter(acc, head_devices):
    if head_devices != 2:
        return lax.psum_scatter(acc, "head", scatter_dimension=1, tiled=True)
    half = acc.shape[1] // 2
    first_half = lax.axis_index("head") == 0
    own = jnp.where(first_half, acc[:, :half], acc[:, half:])
    other = jnp.where(first_half, acc[:, half:], acc[:, :half])
    return own + lax.ppermute(other, "head", [(0, 1), (1, 0)])


def per_device(queries, key_max, key_min, limits, head_devices):
    local_pages = key_max.shape[0]
    kv_count = key_max.shape[1] // DH
    call_count = min(kv_count, GATHERS)
    kv_per_call = kv_count // call_count
    group_cols = queries.shape[1] // call_count
    nb = jnp.stack([jnp.max(limits) // CHUNK + 1, (jnp.min(limits) + 1) // CHUNK]).astype(jnp.int32)
    acc = None
    for g in range(call_count):
        parts = []
        for kv in range(g * kv_per_call, (g + 1) * kv_per_call):
            parts += [key_max[:, kv * DH:(kv + 1) * DH], key_min[:, kv * DH:(kv + 1) * DH]]
        keys = lax.all_gather(jnp.concatenate(parts, axis=1), ("row", "rep"), axis=0, tiled=True)
        acc = page_mass_group(
            nb, queries[:, g * group_cols:(g + 1) * group_cols], keys, limits, acc,
            last=g == call_count - 1)
    return head_sum_scatter(acc, head_devices)


def solution(mesh):
    placed = (
        P(("grp", "row", "rep"), "head"),
        P(("grp", "row", "rep"), "head"),
        P(("grp", "row", "rep"), "head"),
        P(("grp", "row", "rep")),
    )
    return jax.shard_map(
        functools.partial(per_device, head_devices=mesh.shape["head"]),
        mesh=mesh,
        in_specs=placed,
        out_specs=P(("grp", "row", "rep"), "head"),
        check_vma=False,
    )
```

```python
import functools
import math

import jax
import jax.numpy as jnp
from jax import lax
from jax.experimental import pallas as pl
from jax.experimental.pallas import tpu as pltpu
from jax.sharding import PartitionSpec as P

DH = 128
CHUNK = 256
GATHERS = 2
MM_CHUNK = 1024


def _split(x):
    hi = x.astype(jnp.bfloat16)
    lo = (x - hi.astype(jnp.float32)).astype(jnp.bfloat16)
    return hi, lo


def _mass_kernel(nb_ref, q_ref, k_ref, lim_ref, *refs, chunk_count, score_scale, first, last,
                 pairs_per_kv):
    if first:
        out_ref, kcat_ref, s_ref, acc_ref = refs
    else:
        acc_in_ref, out_ref, kcat_ref, s_ref, acc_ref = refs
    hp = pl.program_id(0)
    nb = nb_ref[0]
    nfull = nb_ref[1]
    row_count = q_ref.shape[0]
    lanes = 2 * row_count

    @pl.when(hp == 0)
    def _():
        if first:
            acc_ref[...] = jnp.zeros_like(acc_ref)
        else:
            acc_ref[...] = acc_in_ref[...]

    @pl.when(hp % pairs_per_kv == 0)
    def _():
        for c in range(chunk_count):
            @pl.when(c < nb)
            def _():
                hi, lo = _split(k_ref[c * CHUNK:(c + 1) * CHUNK, :])
                kcat_ref[c * CHUNK:(c + 1) * CHUNK, :] = jnp.concatenate([hi, hi, lo], axis=1)

    q = q_ref[...]
    xs = []
    for j in range(2):
        qj = q[:, j * DH:(j + 1) * DH]
        xs.append(jnp.concatenate([jnp.maximum(qj, 0.0), jnp.minimum(qj, 0.0)], axis=1).T)
    w = jnp.concatenate(xs, axis=1) * score_scale
    whi, wlo = _split(w)
    wcat = jnp.concatenate([whi, wlo, whi], axis=0)
    lim = lim_ref[...]
    lim2 = jnp.concatenate([lim, lim], axis=1)
    page_in_chunk = lax.broadcasted_iota(jnp.int32, (CHUNK, lanes), 0)

    def vreg_fold(v, op):
        return op(v.reshape(CHUNK // 8, 8, lanes), axis=0)

    mm_pages = min(MM_CHUNK, chunk_count * CHUNK)
    for mc in range(chunk_count * CHUNK // mm_pages):
        @pl.when(mc * mm_pages < nb * CHUNK)
        def _():
            s_ref[mc * mm_pages:(mc + 1) * mm_pages, :] = jnp.dot(
                kcat_ref[mc * mm_pages:(mc + 1) * mm_pages, :], wcat,
                preferred_element_type=jnp.float32)

    top = jnp.full((8, lanes), -jnp.inf, jnp.float32)
    for c in range(chunk_count):
        def keep(top):
            return top

        def open_chunk(top, c=c):
            return jnp.maximum(top, vreg_fold(s_ref[c * CHUNK:(c + 1) * CHUNK, :], jnp.max))

        def masked_chunk(top, c=c):
            s = s_ref[c * CHUNK:(c + 1) * CHUNK, :]
            s = jnp.where(page_in_chunk <= lim2 - c * CHUNK, s, -1e30)
            s_ref[c * CHUNK:(c + 1) * CHUNK, :] = s
            return jnp.maximum(top, vreg_fold(s, jnp.max))

        branch = jnp.where(c < nb, jnp.where(c < nfull, 1, 2), 0)
        top = lax.switch(branch, [keep, open_chunk, masked_chunk], top)
    top = jnp.max(top, axis=0, keepdims=True)

    total = jnp.zeros((8, lanes), jnp.float32)
    for c in range(chunk_count):
        def pass_exp(total, c=c):
            e = jnp.exp(s_ref[c * CHUNK:(c + 1) * CHUNK, :] - top)
            s_ref[c * CHUNK:(c + 1) * CHUNK, :] = e
            return total + vreg_fold(e, jnp.sum)
        total = lax.cond(c < nb, pass_exp, lambda t: t, total)
    inv = 1.0 / jnp.sum(total, axis=0, keepdims=True)
    inv_a = inv[:, :row_count]
    inv_b = inv[:, row_count:]

    for c in range(chunk_count):
        @pl.when(c < nb)
        def _():
            e = s_ref[c * CHUNK:(c + 1) * CHUNK, :]
            acc_ref[c * CHUNK:(c + 1) * CHUNK, :] += (
                e[:, :row_count] * inv_a + e[:, row_count:] * inv_b)

    @pl.when(hp == pl.num_programs(0) - 1)
    def _():
        for c in range(chunk_count):
            if last:
                out_ref[:, c * CHUNK:(c + 1) * CHUNK] = acc_ref[c * CHUNK:(c + 1) * CHUNK, :].T
            else:
                out_ref[c * CHUNK:(c + 1) * CHUNK, :] = acc_ref[c * CHUNK:(c + 1) * CHUNK, :]


def page_mass_group(nb, queries, keys, limits, acc, last):
    row_count = queries.shape[0]
    pair_count = queries.shape[1] // (2 * DH)
    pairs_per_kv = pair_count // (keys.shape[1] // (2 * DH))
    page_count = keys.shape[0]
    chunk_count = page_count // CHUNK
    first = acc is None
    kernel = functools.partial(
        _mass_kernel, chunk_count=chunk_count, score_scale=1.0 / math.sqrt(DH),
        first=first, last=last, pairs_per_kv=pairs_per_kv)
    in_specs = [
        pl.BlockSpec((row_count, 2 * DH), lambda hp, nb: (0, hp)),
        pl.BlockSpec((page_count, 2 * DH), lambda hp, nb: (0, hp // pairs_per_kv)),
        pl.BlockSpec((1, row_count), lambda hp, nb: (0, 0)),
    ]
    operands = [nb, queries, keys, limits.reshape(1, row_count)]
    if not first:
        in_specs.append(pl.BlockSpec((page_count, row_count), lambda hp, nb: (0, 0)))
        operands.append(acc)
    if last:
        out_shape = (row_count, page_count)
    else:
        out_shape = (page_count, row_count)
    aliases = {4: 0} if (not first and not last) else {}
    grid_spec = pltpu.PrefetchScalarGridSpec(
        num_scalar_prefetch=1,
        grid=(pair_count,),
        in_specs=in_specs,
        out_specs=pl.BlockSpec(out_shape, lambda hp, nb: (0, 0)),
        scratch_shapes=[
            pltpu.VMEM((page_count, 6 * DH), jnp.bfloat16),
            pltpu.VMEM((page_count, 2 * row_count), jnp.float32),
            pltpu.VMEM((page_count, row_count), jnp.float32),
        ],
    )
    return pl.pallas_call(
        kernel,
        grid_spec=grid_spec,
        out_shape=jax.ShapeDtypeStruct(out_shape, jnp.float32),
        input_output_aliases=aliases,
        compiler_params=pltpu.CompilerParams(dimension_semantics=("arbitrary",)),
    )(*operands)


def head_sum_scatter(acc, head_devices):
    if head_devices != 2:
        return lax.psum_scatter(acc, "head", scatter_dimension=1, tiled=True)
    half = acc.shape[1] // 2
    first_half = lax.axis_index("head") == 0
    own = jnp.where(first_half, acc[:, :half], acc[:, half:])
    other = jnp.where(first_half, acc[:, half:], acc[:, :half])
    return own + lax.ppermute(other, "head", [(0, 1), (1, 0)])


def causal_gather(block, row_devices):
    z = lax.axis_index("row")
    r = lax.axis_index("rep")
    block_pages = block.shape[0]
    forward = [(i, i + 1) for i in range(row_devices - 1)]
    mine = [block]
    for _ in range(1, row_devices):
        mine.append(lax.ppermute(mine[-1], "row", forward))
    mine = jnp.stack(mine)
    sibling = lax.ppermute(mine, "rep", [(0, 1), (1, 0)])
    slots = 2 * row_devices
    out = jnp.zeros((slots * block_pages, block.shape[1]), block.dtype)
    for k in range(row_devices):
        for part, rep_index in ((mine[k], r), (sibling[k], 1 - r)):
            slot = jnp.where(z >= k, 2 * (z - k) + rep_index, slots - 1)
            out = lax.dynamic_update_slice(out, part, (slot * block_pages, 0))
    return out


def per_device(queries, key_max, key_min, limits, head_devices, row_devices):
    local_pages = key_max.shape[0]
    kv_count = key_max.shape[1] // DH
    call_count = min(kv_count, GATHERS)
    kv_per_call = kv_count // call_count
    group_cols = queries.shape[1] // call_count
    nb = jnp.stack([jnp.max(limits) // CHUNK + 1, (jnp.min(limits) + 1) // CHUNK]).astype(jnp.int32)
    acc = None
    for g in range(call_count):
        parts = []
        for kv in range(g * kv_per_call, (g + 1) * kv_per_call):
            parts += [key_max[:, kv * DH:(kv + 1) * DH], key_min[:, kv * DH:(kv + 1) * DH]]
        bounds = jnp.concatenate(parts, axis=1)
        if g == 0:
            keys = lax.all_gather(bounds, ("row", "rep"), axis=0, tiled=True)
        else:
            keys = causal_gather(bounds, row_devices)
        acc = page_mass_group(
            nb, queries[:, g * group_cols:(g + 1) * group_cols], keys, limits, acc,
            last=g == call_count - 1)
    return head_sum_scatter(acc, head_devices)


def solution(mesh):
    placed = (
        P(("grp", "row", "rep"), "head"),
        P(("grp", "row", "rep"), "head"),
        P(("grp", "row", "rep"), "head"),
        P(("grp", "row", "rep")),
    )
    return jax.shard_map(
        functools.partial(
            per_device, head_devices=mesh.shape["head"], row_devices=mesh.shape["row"]),
        mesh=mesh,
        in_specs=placed,
        out_specs=P(("grp", "row", "rep"), "head"),
        check_vma=False,
    )
```

```python
import functools
import math

import jax
import jax.numpy as jnp
from jax import lax
from jax.experimental import pallas as pl
from jax.experimental.pallas import tpu as pltpu
from jax.sharding import PartitionSpec as P

DH = 128
CHUNK = 256
MM_CHUNK = 1024


def _split(x):
    hi = x.astype(jnp.bfloat16)
    lo = (x - hi.astype(jnp.float32)).astype(jnp.bfloat16)
    return hi, lo


def _mass_kernel(nb_ref, q_ref, k_ref, lim_ref, *refs, chunk_count, score_scale, first, last,
                 pairs_per_kv):
    if first:
        out_ref, kcat_ref, s_ref, acc_ref = refs
    else:
        acc_in_ref, out_ref, kcat_ref, s_ref, acc_ref = refs
    hp = pl.program_id(0)
    nb = nb_ref[0]
    nfull = nb_ref[1]
    row_count = q_ref.shape[0]
    lanes = 2 * row_count

    @pl.when(hp == 0)
    def _():
        if first:
            acc_ref[...] = jnp.zeros_like(acc_ref)
        else:
            acc_ref[...] = acc_in_ref[...]

    @pl.when(hp % pairs_per_kv == 0)
    def _():
        for c in range(chunk_count):
            @pl.when(c < nb)
            def _():
                hi, lo = _split(k_ref[c * CHUNK:(c + 1) * CHUNK, :])
                kcat_ref[c * CHUNK:(c + 1) * CHUNK, :] = jnp.concatenate([hi, hi, lo], axis=1)

    q = q_ref[...]
    xs = []
    for j in range(2):
        qj = q[:, j * DH:(j + 1) * DH]
        xs.append(jnp.concatenate([jnp.maximum(qj, 0.0), jnp.minimum(qj, 0.0)], axis=1).T)
    w = jnp.concatenate(xs, axis=1) * score_scale
    whi, wlo = _split(w)
    wcat = jnp.concatenate([whi, wlo, whi], axis=0)
    lim = lim_ref[...]
    lim2 = jnp.concatenate([lim, lim], axis=1)
    page_in_chunk = lax.broadcasted_iota(jnp.int32, (CHUNK, lanes), 0)

    def vreg_fold(v, op):
        return op(v.reshape(CHUNK // 8, 8, lanes), axis=0)

    mm_pages = min(MM_CHUNK, chunk_count * CHUNK)
    for mc in range(chunk_count * CHUNK // mm_pages):
        @pl.when(mc * mm_pages < nb * CHUNK)
        def _():
            s_ref[mc * mm_pages:(mc + 1) * mm_pages, :] = jnp.dot(
                kcat_ref[mc * mm_pages:(mc + 1) * mm_pages, :], wcat,
                preferred_element_type=jnp.float32)

    top = jnp.full((8, lanes), -jnp.inf, jnp.float32)
    for c in range(chunk_count):
        def keep(top):
            return top

        def open_chunk(top, c=c):
            return jnp.maximum(top, vreg_fold(s_ref[c * CHUNK:(c + 1) * CHUNK, :], jnp.max))

        def masked_chunk(top, c=c):
            s = s_ref[c * CHUNK:(c + 1) * CHUNK, :]
            s = jnp.where(page_in_chunk <= lim2 - c * CHUNK, s, -1e30)
            s_ref[c * CHUNK:(c + 1) * CHUNK, :] = s
            return jnp.maximum(top, vreg_fold(s, jnp.max))

        branch = jnp.where(c < nb, jnp.where(c < nfull, 1, 2), 0)
        top = lax.switch(branch, [keep, open_chunk, masked_chunk], top)
    top = jnp.max(top, axis=0, keepdims=True)

    total = jnp.zeros((8, lanes), jnp.float32)
    for c in range(chunk_count):
        def pass_exp(total, c=c):
            e = jnp.exp(s_ref[c * CHUNK:(c + 1) * CHUNK, :] - top)
            s_ref[c * CHUNK:(c + 1) * CHUNK, :] = e
            return total + vreg_fold(e, jnp.sum)
        total = lax.cond(c < nb, pass_exp, lambda t: t, total)
    inv = 1.0 / jnp.sum(total, axis=0, keepdims=True)
    inv_a = inv[:, :row_count]
    inv_b = inv[:, row_count:]

    for c in range(chunk_count):
        @pl.when(c < nb)
        def _():
            e = s_ref[c * CHUNK:(c + 1) * CHUNK, :]
            acc_ref[c * CHUNK:(c + 1) * CHUNK, :] += (
                e[:, :row_count] * inv_a + e[:, row_count:] * inv_b)

    @pl.when(hp == pl.num_programs(0) - 1)
    def _():
        for c in range(chunk_count):
            if last:
                out_ref[:, c * CHUNK:(c + 1) * CHUNK] = acc_ref[c * CHUNK:(c + 1) * CHUNK, :].T
            else:
                out_ref[c * CHUNK:(c + 1) * CHUNK, :] = acc_ref[c * CHUNK:(c + 1) * CHUNK, :]


def page_mass_group(nb, queries, keys, limits, acc, last):
    row_count = queries.shape[0]
    pair_count = queries.shape[1] // (2 * DH)
    pairs_per_kv = pair_count // (keys.shape[1] // (2 * DH))
    page_count = keys.shape[0]
    chunk_count = page_count // CHUNK
    first = acc is None
    kernel = functools.partial(
        _mass_kernel, chunk_count=chunk_count, score_scale=1.0 / math.sqrt(DH),
        first=first, last=last, pairs_per_kv=pairs_per_kv)
    in_specs = [
        pl.BlockSpec((row_count, 2 * DH), lambda hp, nb: (0, hp)),
        pl.BlockSpec((page_count, 2 * DH), lambda hp, nb: (0, hp // pairs_per_kv)),
        pl.BlockSpec((1, row_count), lambda hp, nb: (0, 0)),
    ]
    operands = [nb, queries, keys, limits.reshape(1, row_count)]
    if not first:
        in_specs.append(pl.BlockSpec((page_count, row_count), lambda hp, nb: (0, 0)))
        operands.append(acc)
    if last:
        out_shape = (row_count, page_count)
    else:
        out_shape = (page_count, row_count)
    aliases = {4: 0} if (not first and not last) else {}
    grid_spec = pltpu.PrefetchScalarGridSpec(
        num_scalar_prefetch=1,
        grid=(pair_count,),
        in_specs=in_specs,
        out_specs=pl.BlockSpec(out_shape, lambda hp, nb: (0, 0)),
        scratch_shapes=[
            pltpu.VMEM((page_count, 6 * DH), jnp.bfloat16),
            pltpu.VMEM((page_count, 2 * row_count), jnp.float32),
            pltpu.VMEM((page_count, row_count), jnp.float32),
        ],
    )
    return pl.pallas_call(
        kernel,
        grid_spec=grid_spec,
        out_shape=jax.ShapeDtypeStruct(out_shape, jnp.float32),
        input_output_aliases=aliases,
        compiler_params=pltpu.CompilerParams(dimension_semantics=("arbitrary",)),
    )(*operands)


def head_sum_scatter(acc, head_devices):
    if head_devices != 2:
        return lax.psum_scatter(acc, "head", scatter_dimension=1, tiled=True)
    half = acc.shape[1] // 2
    first_half = lax.axis_index("head") == 0
    own = jnp.where(first_half, acc[:, :half], acc[:, half:])
    other = jnp.where(first_half, acc[:, half:], acc[:, :half])
    return own + lax.ppermute(other, "head", [(0, 1), (1, 0)])


def per_device(queries, key_max, key_min, limits, head_devices):
    local_pages = key_max.shape[0]
    kv_count = key_max.shape[1] // DH
    head_cols = queries.shape[1] // kv_count
    sizes = [kv_count - 1, 1] if kv_count > 1 else [kv_count]
    nb = jnp.stack([jnp.max(limits) // CHUNK + 1, (jnp.min(limits) + 1) // CHUNK]).astype(jnp.int32)
    acc = None
    kv0 = 0
    for g, size in enumerate(sizes):
        parts = []
        for kv in range(kv0, kv0 + size):
            parts += [key_max[:, kv * DH:(kv + 1) * DH], key_min[:, kv * DH:(kv + 1) * DH]]
        keys = lax.all_gather(jnp.concatenate(parts, axis=1), ("row", "rep"), axis=0, tiled=True)
        cols = slice(kv0 * head_cols, (kv0 + size) * head_cols)
        acc = page_mass_group(nb, queries[:, cols], keys, limits, acc, last=g == len(sizes) - 1)
        kv0 += size
    return head_sum_scatter(acc, head_devices)


def solution(mesh):
    placed = (
        P(("grp", "row", "rep"), "head"),
        P(("grp", "row", "rep"), "head"),
        P(("grp", "row", "rep"), "head"),
        P(("grp", "row", "rep")),
    )
    return jax.shard_map(
        functools.partial(per_device, head_devices=mesh.shape["head"]),
        mesh=mesh,
        in_specs=placed,
        out_specs=P(("grp", "row", "rep"), "head"),
        check_vma=False,
    )
```

```python
import functools
import math

import jax
import jax.numpy as jnp
from jax import lax
from jax.experimental import pallas as pl
from jax.experimental.pallas import tpu as pltpu
from jax.sharding import PartitionSpec as P

DH = 128
CHUNK = 256
MM_CHUNK = 1024


def _split(x):
    hi = x.astype(jnp.bfloat16)
    lo = (x - hi.astype(jnp.float32)).astype(jnp.bfloat16)
    return hi, lo


def _mass_kernel(nb_ref, q_ref, k_ref, lim_ref, *refs, chunk_count, score_scale, first, last,
                 pairs_per_kv):
    if first:
        out_ref, kcat_ref, s_ref, acc_ref, tops_ref = refs
    else:
        acc_in_ref, out_ref, kcat_ref, s_ref, acc_ref, tops_ref = refs
    hp = pl.program_id(0)
    nb = nb_ref[0]
    nfull = nb_ref[1]
    row_count = q_ref.shape[0]
    lanes = 2 * row_count

    @pl.when(hp == 0)
    def _():
        if first:
            acc_ref[...] = jnp.zeros_like(acc_ref)
        else:
            acc_ref[...] = acc_in_ref[...]

    @pl.when(hp % pairs_per_kv == 0)
    def _():
        for c in range(chunk_count):
            @pl.when(c < nb)
            def _():
                hi, lo = _split(k_ref[c * CHUNK:(c + 1) * CHUNK, :])
                kcat_ref[c * CHUNK:(c + 1) * CHUNK, :] = jnp.concatenate([hi, hi, lo], axis=1)

    q = q_ref[...]
    xs = []
    for j in range(2):
        qj = q[:, j * DH:(j + 1) * DH]
        xs.append(jnp.concatenate([jnp.maximum(qj, 0.0), jnp.minimum(qj, 0.0)], axis=1).T)
    w = jnp.concatenate(xs, axis=1) * score_scale
    whi, wlo = _split(w)
    wcat = jnp.concatenate([whi, wlo, whi], axis=0)
    lim = lim_ref[...]
    lim2 = jnp.concatenate([lim, lim], axis=1)
    page_in_chunk = lax.broadcasted_iota(jnp.int32, (CHUNK, lanes), 0)

    def vreg_fold(v, op):
        return op(v.reshape(CHUNK // 8, 8, lanes), axis=0)

    mm_pages = min(MM_CHUNK, chunk_count * CHUNK)
    per_mm = mm_pages // CHUNK
    for mc in range(chunk_count * CHUNK // mm_pages):
        @pl.when(mc * mm_pages < nb * CHUNK)
        def _():
            s = jnp.dot(kcat_ref[mc * mm_pages:(mc + 1) * mm_pages, :], wcat,
                        preferred_element_type=jnp.float32)
            s_ref[mc * mm_pages:(mc + 1) * mm_pages, :] = s
            for j in range(per_mm):
                c = mc * per_mm + j
                tops_ref[c * 8:(c + 1) * 8, :] = vreg_fold(s[j * CHUNK:(j + 1) * CHUNK, :], jnp.max)

    top = jnp.full((8, lanes), -jnp.inf, jnp.float32)
    for c in range(chunk_count):
        def keep(top):
            return top

        def open_chunk(top, c=c):
            return jnp.maximum(top, tops_ref[c * 8:(c + 1) * 8, :])

        def masked_chunk(top, c=c):
            s = s_ref[c * CHUNK:(c + 1) * CHUNK, :]
            s = jnp.where(page_in_chunk <= lim2 - c * CHUNK, s, -1e30)
            s_ref[c * CHUNK:(c + 1) * CHUNK, :] = s
            return jnp.maximum(top, vreg_fold(s, jnp.max))

        branch = jnp.where(c < nb, jnp.where(c < nfull, 1, 2), 0)
        top = lax.switch(branch, [keep, open_chunk, masked_chunk], top)
    top = jnp.max(top, axis=0, keepdims=True)

    total = jnp.zeros((8, lanes), jnp.float32)
    for c in range(chunk_count):
        def pass_exp(total, c=c):
            e = jnp.exp2(s_ref[c * CHUNK:(c + 1) * CHUNK, :] - top)
            s_ref[c * CHUNK:(c + 1) * CHUNK, :] = e
            return total + vreg_fold(e, jnp.sum)
        total = lax.cond(c < nb, pass_exp, lambda t: t, total)
    inv = 1.0 / jnp.sum(total, axis=0, keepdims=True)
    inv_a = inv[:, :row_count]
    inv_b = inv[:, row_count:]

    for c in range(chunk_count):
        @pl.when(c < nb)
        def _():
            e = s_ref[c * CHUNK:(c + 1) * CHUNK, :]
            acc_ref[c * CHUNK:(c + 1) * CHUNK, :] += (
                e[:, :row_count] * inv_a + e[:, row_count:] * inv_b)

    @pl.when(hp == pl.num_programs(0) - 1)
    def _():
        for c in range(chunk_count):
            if last:
                out_ref[:, c * CHUNK:(c + 1) * CHUNK] = acc_ref[c * CHUNK:(c + 1) * CHUNK, :].T
            else:
                out_ref[c * CHUNK:(c + 1) * CHUNK, :] = acc_ref[c * CHUNK:(c + 1) * CHUNK, :]


def page_mass_group(nb, queries, keys, limits, acc, last):
    row_count = queries.shape[0]
    pair_count = queries.shape[1] // (2 * DH)
    pairs_per_kv = pair_count // (keys.shape[1] // (2 * DH))
    page_count = keys.shape[0]
    chunk_count = page_count // CHUNK
    first = acc is None
    kernel = functools.partial(
        _mass_kernel, chunk_count=chunk_count, score_scale=math.log2(math.e) / math.sqrt(DH),
        first=first, last=last, pairs_per_kv=pairs_per_kv)
    in_specs = [
        pl.BlockSpec((row_count, 2 * DH), lambda hp, nb: (0, hp)),
        pl.BlockSpec((page_count, 2 * DH), lambda hp, nb: (0, hp // pairs_per_kv)),
        pl.BlockSpec((1, row_count), lambda hp, nb: (0, 0)),
    ]
    operands = [nb, queries, keys, limits.reshape(1, row_count)]
    if not first:
        in_specs.append(pl.BlockSpec((page_count, row_count), lambda hp, nb: (0, 0)))
        operands.append(acc)
    if last:
        out_shape = (row_count, page_count)
    else:
        out_shape = (page_count, row_count)
    aliases = {4: 0} if (not first and not last) else {}
    grid_spec = pltpu.PrefetchScalarGridSpec(
        num_scalar_prefetch=1,
        grid=(pair_count,),
        in_specs=in_specs,
        out_specs=pl.BlockSpec(out_shape, lambda hp, nb: (0, 0)),
        scratch_shapes=[
            pltpu.VMEM((page_count, 6 * DH), jnp.bfloat16),
            pltpu.VMEM((page_count, 2 * row_count), jnp.float32),
            pltpu.VMEM((page_count, row_count), jnp.float32),
            pltpu.VMEM((chunk_count * 8, 2 * row_count), jnp.float32),
        ],
    )
    return pl.pallas_call(
        kernel,
        grid_spec=grid_spec,
        out_shape=jax.ShapeDtypeStruct(out_shape, jnp.float32),
        input_output_aliases=aliases,
        compiler_params=pltpu.CompilerParams(dimension_semantics=("arbitrary",)),
    )(*operands)


def head_sum_scatter(acc, head_devices):
    if head_devices != 2:
        return lax.psum_scatter(acc, "head", scatter_dimension=1, tiled=True)
    half = acc.shape[1] // 2
    first_half = lax.axis_index("head") == 0
    own = jnp.where(first_half, acc[:, :half], acc[:, half:])
    other = jnp.where(first_half, acc[:, half:], acc[:, :half])
    return own + lax.ppermute(other, "head", [(0, 1), (1, 0)])


def per_device(queries, key_max, key_min, limits, head_devices):
    local_pages = key_max.shape[0]
    kv_count = key_max.shape[1] // DH
    head_cols = queries.shape[1] // kv_count
    sizes = [kv_count - 1, 1] if kv_count > 1 else [kv_count]
    nb = jnp.stack([jnp.max(limits) // CHUNK + 1, (jnp.min(limits) + 1) // CHUNK]).astype(jnp.int32)
    acc = None
    kv0 = 0
    for g, size in enumerate(sizes):
        parts = []
        for kv in range(kv0, kv0 + size):
            parts += [key_max[:, kv * DH:(kv + 1) * DH], key_min[:, kv * DH:(kv + 1) * DH]]
        keys = lax.all_gather(jnp.concatenate(parts, axis=1), ("row", "rep"), axis=0, tiled=True)
        cols = slice(kv0 * head_cols, (kv0 + size) * head_cols)
        acc = page_mass_group(nb, queries[:, cols], keys, limits, acc, last=g == len(sizes) - 1)
        kv0 += size
    return head_sum_scatter(acc, head_devices)


def solution(mesh):
    placed = (
        P(("grp", "row", "rep"), "head"),
        P(("grp", "row", "rep"), "head"),
        P(("grp", "row", "rep"), "head"),
        P(("grp", "row", "rep")),
    )
    return jax.shard_map(
        functools.partial(per_device, head_devices=mesh.shape["head"]),
        mesh=mesh,
        in_specs=placed,
        out_specs=P(("grp", "row", "rep"), "head"),
        check_vma=False,
    )
```

```python
import functools
import math

import jax
import jax.numpy as jnp
from jax import lax
from jax.experimental import pallas as pl
from jax.experimental.pallas import tpu as pltpu
from jax.sharding import PartitionSpec as P

DH = 128
CHUNK = 256
MM_CHUNK = 1024


def _split(x):
    hi = x.astype(jnp.bfloat16)
    lo = (x - hi.astype(jnp.float32)).astype(jnp.bfloat16)
    return hi, lo


def _mass_kernel(nb_ref, q_ref, k_ref, lim_ref, *refs, chunk_count, score_scale, first, last,
                 pairs_per_kv):
    if first:
        out_ref, kcat_ref, s_ref, acc_ref, tops_ref = refs
    else:
        acc_in_ref, out_ref, kcat_ref, s_ref, acc_ref, tops_ref = refs
    hp = pl.program_id(0)
    nb = nb_ref[0]
    nfull = nb_ref[1]
    row_count = q_ref.shape[0]
    lanes = 2 * row_count

    @pl.when(hp == 0)
    def _():
        if first:
            acc_ref[...] = jnp.zeros_like(acc_ref)
        else:
            acc_ref[...] = acc_in_ref[...]

    @pl.when(hp % pairs_per_kv == 0)
    def _():
        for c in range(chunk_count):
            @pl.when(c < nb)
            def _():
                hi, lo = _split(k_ref[c * CHUNK:(c + 1) * CHUNK, :])
                kcat_ref[c * CHUNK:(c + 1) * CHUNK, :] = jnp.concatenate([hi, hi, lo], axis=1)

    q = q_ref[...]
    xs = []
    for j in range(2):
        qj = q[:, j * DH:(j + 1) * DH]
        xs.append(jnp.concatenate([jnp.maximum(qj, 0.0), jnp.minimum(qj, 0.0)], axis=1).T)
    w = jnp.concatenate(xs, axis=1) * score_scale
    whi, wlo = _split(w)
    wcat = jnp.concatenate([whi, wlo, whi], axis=0)
    lim = lim_ref[...]
    lim2 = jnp.concatenate([lim, lim], axis=1)
    page_in_chunk = lax.broadcasted_iota(jnp.int32, (CHUNK, lanes), 0)

    def vreg_fold(v, op):
        return op(v.reshape(CHUNK // 8, 8, lanes), axis=0)

    mm_pages = min(MM_CHUNK, chunk_count * CHUNK)
    per_mm = mm_pages // CHUNK
    for mc in range(chunk_count * CHUNK // mm_pages):
        @pl.when(mc * mm_pages < nb * CHUNK)
        def _():
            s = jnp.dot(kcat_ref[mc * mm_pages:(mc + 1) * mm_pages, :], wcat,
                        preferred_element_type=jnp.float32)
            s_ref[mc * mm_pages:(mc + 1) * mm_pages, :] = s
            for j in range(per_mm):
                c = mc * per_mm + j
                tops_ref[c * 8:(c + 1) * 8, :] = vreg_fold(s[j * CHUNK:(j + 1) * CHUNK, :], jnp.max)

    top = jnp.full((8, lanes), -jnp.inf, jnp.float32)
    for c in range(chunk_count):
        def keep(top):
            return top

        def open_chunk(top, c=c):
            return jnp.maximum(top, tops_ref[c * 8:(c + 1) * 8, :])

        def masked_chunk(top, c=c):
            s = s_ref[c * CHUNK:(c + 1) * CHUNK, :]
            s = jnp.where(page_in_chunk <= lim2 - c * CHUNK, s, -1e30)
            s_ref[c * CHUNK:(c + 1) * CHUNK, :] = s
            return jnp.maximum(top, vreg_fold(s, jnp.max))

        branch = jnp.where(c < nb, jnp.where(c < nfull, 1, 2), 0)
        top = lax.switch(branch, [keep, open_chunk, masked_chunk], top)
    top = jnp.max(top, axis=0, keepdims=True)

    total = jnp.zeros((8, lanes), jnp.float32)
    for c in range(chunk_count):
        def pass_exp(total, c=c):
            e = jnp.exp2(s_ref[c * CHUNK:(c + 1) * CHUNK, :] - top)
            s_ref[c * CHUNK:(c + 1) * CHUNK, :] = e
            return total + vreg_fold(e, jnp.sum)
        total = lax.cond(c < nb, pass_exp, lambda t: t, total)
    inv = 1.0 / jnp.sum(total, axis=0, keepdims=True)
    inv_a = inv[:, :row_count]
    inv_b = inv[:, row_count:]

    for c in range(chunk_count):
        @pl.when(c < nb)
        def _():
            e = s_ref[c * CHUNK:(c + 1) * CHUNK, :]
            acc_ref[c * CHUNK:(c + 1) * CHUNK, :] += (
                e[:, :row_count] * inv_a + e[:, row_count:] * inv_b)

    @pl.when(hp == pl.num_programs(0) - 1)
    def _():
        for c in range(chunk_count):
            if last:
                out_ref[:, c * CHUNK:(c + 1) * CHUNK] = acc_ref[c * CHUNK:(c + 1) * CHUNK, :].T
            else:
                out_ref[c * CHUNK:(c + 1) * CHUNK, :] = acc_ref[c * CHUNK:(c + 1) * CHUNK, :]


def page_mass_group(nb, queries, keys, limits, acc, last):
    row_count = queries.shape[0]
    pair_count = queries.shape[1] // (2 * DH)
    pairs_per_kv = pair_count // (keys.shape[1] // (2 * DH))
    page_count = keys.shape[0]
    chunk_count = page_count // CHUNK
    first = acc is None
    kernel = functools.partial(
        _mass_kernel, chunk_count=chunk_count, score_scale=math.log2(math.e) / math.sqrt(DH),
        first=first, last=last, pairs_per_kv=pairs_per_kv)
    in_specs = [
        pl.BlockSpec((row_count, 2 * DH), lambda hp, nb: (0, hp)),
        pl.BlockSpec((page_count, 2 * DH), lambda hp, nb: (0, hp // pairs_per_kv)),
        pl.BlockSpec((1, row_count), lambda hp, nb: (0, 0)),
    ]
    operands = [nb, queries, keys, limits.reshape(1, row_count)]
    if not first:
        in_specs.append(pl.BlockSpec((page_count, row_count), lambda hp, nb: (0, 0)))
        operands.append(acc)
    if last:
        out_shape = (row_count, page_count)
    else:
        out_shape = (page_count, row_count)
    aliases = {4: 0} if (not first and not last) else {}
    grid_spec = pltpu.PrefetchScalarGridSpec(
        num_scalar_prefetch=1,
        grid=(pair_count,),
        in_specs=in_specs,
        out_specs=pl.BlockSpec(out_shape, lambda hp, nb: (0, 0)),
        scratch_shapes=[
            pltpu.VMEM((page_count, 6 * DH), jnp.bfloat16),
            pltpu.VMEM((page_count, 2 * row_count), jnp.float32),
            pltpu.VMEM((page_count, row_count), jnp.float32),
            pltpu.VMEM((chunk_count * 8, 2 * row_count), jnp.float32),
        ],
    )
    return pl.pallas_call(
        kernel,
        grid_spec=grid_spec,
        out_shape=jax.ShapeDtypeStruct(out_shape, jnp.float32),
        input_output_aliases=aliases,
        compiler_params=pltpu.CompilerParams(dimension_semantics=("arbitrary",)),
    )(*operands)


def head_sum_scatter(acc, head_devices):
    if head_devices != 2:
        return lax.psum_scatter(acc, "head", scatter_dimension=1, tiled=True)
    half = acc.shape[1] // 2
    first_half = lax.axis_index("head") == 0
    own = jnp.where(first_half, acc[:, :half], acc[:, half:])
    other = jnp.where(first_half, acc[:, half:], acc[:, :half])
    return own + lax.ppermute(other, "head", [(0, 1), (1, 0)])


def gather_blocks(block):
    devices = lax.psum(1, ("row", "rep"))
    copies = jnp.broadcast_to(block[None], (devices,) + block.shape)
    got = lax.all_to_all(copies, ("row", "rep"), 0, 0, tiled=True)
    return got.reshape(devices * block.shape[0], block.shape[1])


def per_device(queries, key_max, key_min, limits, head_devices):
    local_pages = key_max.shape[0]
    kv_count = key_max.shape[1] // DH
    head_cols = queries.shape[1] // kv_count
    sizes = [kv_count - 1, 1] if kv_count > 1 else [kv_count]
    nb = jnp.stack([jnp.max(limits) // CHUNK + 1, (jnp.min(limits) + 1) // CHUNK]).astype(jnp.int32)
    acc = None
    kv0 = 0
    for g, size in enumerate(sizes):
        parts = []
        for kv in range(kv0, kv0 + size):
            parts += [key_max[:, kv * DH:(kv + 1) * DH], key_min[:, kv * DH:(kv + 1) * DH]]
        keys = gather_blocks(jnp.concatenate(parts, axis=1))
        cols = slice(kv0 * head_cols, (kv0 + size) * head_cols)
        acc = page_mass_group(nb, queries[:, cols], keys, limits, acc, last=g == len(sizes) - 1)
        kv0 += size
    return head_sum_scatter(acc, head_devices)


def solution(mesh):
    placed = (
        P(("grp", "row", "rep"), "head"),
        P(("grp", "row", "rep"), "head"),
        P(("grp", "row", "rep"), "head"),
        P(("grp", "row", "rep")),
    )
    return jax.shard_map(
        functools.partial(per_device, head_devices=mesh.shape["head"]),
        mesh=mesh,
        in_specs=placed,
        out_specs=P(("grp", "row", "rep"), "head"),
        check_vma=False,
    )
```

```python
import functools
import math

import jax
import jax.numpy as jnp
from jax import lax
from jax.experimental import pallas as pl
from jax.experimental.pallas import tpu as pltpu
from jax.sharding import PartitionSpec as P

DH = 128
CHUNK = 256
MM_CHUNK = 1024
HEAD_SUM_PIECES = 4


def _split(x):
    hi = x.astype(jnp.bfloat16)
    lo = (x - hi.astype(jnp.float32)).astype(jnp.bfloat16)
    return hi, lo


def _mass_kernel(nb_ref, q_ref, k_ref, lim_ref, *refs, chunk_count, score_scale, first, last,
                 pairs_per_kv):
    if first:
        out_ref, kcat_ref, s_ref, acc_ref, tops_ref = refs
    else:
        acc_in_ref, out_ref, kcat_ref, s_ref, acc_ref, tops_ref = refs
    hp = pl.program_id(0)
    nb = nb_ref[0]
    nfull = nb_ref[1]
    row_count = q_ref.shape[0]
    lanes = 2 * row_count

    @pl.when(hp == 0)
    def _():
        if first:
            acc_ref[...] = jnp.zeros_like(acc_ref)
        else:
            acc_ref[...] = acc_in_ref[...]

    @pl.when(hp % pairs_per_kv == 0)
    def _():
        for c in range(chunk_count):
            @pl.when(c < nb)
            def _():
                hi, lo = _split(k_ref[c * CHUNK:(c + 1) * CHUNK, :])
                kcat_ref[c * CHUNK:(c + 1) * CHUNK, :] = jnp.concatenate([hi, hi, lo], axis=1)

    q = q_ref[...]
    xs = []
    for j in range(2):
        qj = q[:, j * DH:(j + 1) * DH]
        xs.append(jnp.concatenate([jnp.maximum(qj, 0.0), jnp.minimum(qj, 0.0)], axis=1).T)
    w = jnp.concatenate(xs, axis=1) * score_scale
    whi, wlo = _split(w)
    wcat = jnp.concatenate([whi, wlo, whi], axis=0)
    lim = lim_ref[...]
    lim2 = jnp.concatenate([lim, lim], axis=1)
    page_in_chunk = lax.broadcasted_iota(jnp.int32, (CHUNK, lanes), 0)

    def vreg_fold(v, op):
        return op(v.reshape(CHUNK // 8, 8, lanes), axis=0)

    mm_pages = min(MM_CHUNK, chunk_count * CHUNK)
    per_mm = mm_pages // CHUNK
    for mc in range(chunk_count * CHUNK // mm_pages):
        @pl.when(mc * mm_pages < nb * CHUNK)
        def _():
            s = jnp.dot(kcat_ref[mc * mm_pages:(mc + 1) * mm_pages, :], wcat,
                        preferred_element_type=jnp.float32)
            s_ref[mc * mm_pages:(mc + 1) * mm_pages, :] = s
            for j in range(per_mm):
                c = mc * per_mm + j
                tops_ref[c * 8:(c + 1) * 8, :] = vreg_fold(s[j * CHUNK:(j + 1) * CHUNK, :], jnp.max)

    top = jnp.full((8, lanes), -jnp.inf, jnp.float32)
    for c in range(chunk_count):
        def keep(top):
            return top

        def open_chunk(top, c=c):
            return jnp.maximum(top, tops_ref[c * 8:(c + 1) * 8, :])

        def masked_chunk(top, c=c):
            s = s_ref[c * CHUNK:(c + 1) * CHUNK, :]
            s = jnp.where(page_in_chunk <= lim2 - c * CHUNK, s, -1e30)
            s_ref[c * CHUNK:(c + 1) * CHUNK, :] = s
            return jnp.maximum(top, vreg_fold(s, jnp.max))

        branch = jnp.where(c < nb, jnp.where(c < nfull, 1, 2), 0)
        top = lax.switch(branch, [keep, open_chunk, masked_chunk], top)
    top = jnp.max(top, axis=0, keepdims=True)

    total = jnp.zeros((8, lanes), jnp.float32)
    for c in range(chunk_count):
        def pass_exp(total, c=c):
            e = jnp.exp2(s_ref[c * CHUNK:(c + 1) * CHUNK, :] - top)
            s_ref[c * CHUNK:(c + 1) * CHUNK, :] = e
            return total + vreg_fold(e, jnp.sum)
        total = lax.cond(c < nb, pass_exp, lambda t: t, total)
    inv = 1.0 / jnp.sum(total, axis=0, keepdims=True)
    inv_a = inv[:, :row_count]
    inv_b = inv[:, row_count:]

    for c in range(chunk_count):
        @pl.when(c < nb)
        def _():
            e = s_ref[c * CHUNK:(c + 1) * CHUNK, :]
            acc_ref[c * CHUNK:(c + 1) * CHUNK, :] += (
                e[:, :row_count] * inv_a + e[:, row_count:] * inv_b)

    @pl.when(hp == pl.num_programs(0) - 1)
    def _():
        for c in range(chunk_count):
            if last:
                out_ref[:, c * CHUNK:(c + 1) * CHUNK] = acc_ref[c * CHUNK:(c + 1) * CHUNK, :].T
            else:
                out_ref[c * CHUNK:(c + 1) * CHUNK, :] = acc_ref[c * CHUNK:(c + 1) * CHUNK, :]


def page_mass_group(nb, queries, keys, limits, acc, last):
    row_count = queries.shape[0]
    pair_count = queries.shape[1] // (2 * DH)
    pairs_per_kv = pair_count // (keys.shape[1] // (2 * DH))
    page_count = keys.shape[0]
    chunk_count = page_count // CHUNK
    first = acc is None
    kernel = functools.partial(
        _mass_kernel, chunk_count=chunk_count, score_scale=math.log2(math.e) / math.sqrt(DH),
        first=first, last=last, pairs_per_kv=pairs_per_kv)
    in_specs = [
        pl.BlockSpec((row_count, 2 * DH), lambda hp, nb: (0, hp)),
        pl.BlockSpec((page_count, 2 * DH), lambda hp, nb: (0, hp // pairs_per_kv)),
        pl.BlockSpec((1, row_count), lambda hp, nb: (0, 0)),
    ]
    operands = [nb, queries, keys, limits.reshape(1, row_count)]
    if not first:
        in_specs.append(pl.BlockSpec((page_count, row_count), lambda hp, nb: (0, 0)))
        operands.append(acc)
    if last:
        out_shape = (row_count, page_count)
    else:
        out_shape = (page_count, row_count)
    aliases = {4: 0} if (not first and not last) else {}
    grid_spec = pltpu.PrefetchScalarGridSpec(
        num_scalar_prefetch=1,
        grid=(pair_count,),
        in_specs=in_specs,
        out_specs=pl.BlockSpec(out_shape, lambda hp, nb: (0, 0)),
        scratch_shapes=[
            pltpu.VMEM((page_count, 6 * DH), jnp.bfloat16),
            pltpu.VMEM((page_count, 2 * row_count), jnp.float32),
            pltpu.VMEM((page_count, row_count), jnp.float32),
            pltpu.VMEM((chunk_count * 8, 2 * row_count), jnp.float32),
        ],
    )
    return pl.pallas_call(
        kernel,
        grid_spec=grid_spec,
        out_shape=jax.ShapeDtypeStruct(out_shape, jnp.float32),
        input_output_aliases=aliases,
        compiler_params=pltpu.CompilerParams(dimension_semantics=("arbitrary",)),
    )(*operands)


def head_sum_scatter(acc, head_devices):
    if head_devices != 2:
        return lax.psum_scatter(acc, "head", scatter_dimension=1, tiled=True)
    half = acc.shape[1] // 2
    first_half = lax.axis_index("head") == 0
    own = jnp.where(first_half, acc[:, :half], acc[:, half:])
    other = jnp.where(first_half, acc[:, half:], acc[:, :half])
    pieces = jnp.split(other, HEAD_SUM_PIECES, axis=0)
    sent = [lax.ppermute(p, "head", [(0, 1), (1, 0)]) for p in pieces]
    return own + jnp.concatenate(sent, axis=0)


def per_device(queries, key_max, key_min, limits, head_devices):
    local_pages = key_max.shape[0]
    kv_count = key_max.shape[1] // DH
    head_cols = queries.shape[1] // kv_count
    sizes = [kv_count - 1, 1] if kv_count > 1 else [kv_count]
    nb = jnp.stack([jnp.max(limits) // CHUNK + 1, (jnp.min(limits) + 1) // CHUNK]).astype(jnp.int32)
    acc = None
    kv0 = 0
    for g, size in enumerate(sizes):
        parts = []
        for kv in range(kv0, kv0 + size):
            parts += [key_max[:, kv * DH:(kv + 1) * DH], key_min[:, kv * DH:(kv + 1) * DH]]
        keys = lax.all_gather(jnp.concatenate(parts, axis=1), ("row", "rep"), axis=0, tiled=True)
        cols = slice(kv0 * head_cols, (kv0 + size) * head_cols)
        acc = page_mass_group(nb, queries[:, cols], keys, limits, acc, last=g == len(sizes) - 1)
        kv0 += size
    return head_sum_scatter(acc, head_devices)


def solution(mesh):
    placed = (
        P(("grp", "row", "rep"), "head"),
        P(("grp", "row", "rep"), "head"),
        P(("grp", "row", "rep"), "head"),
        P(("grp", "row", "rep")),
    )
    return jax.shard_map(
        functools.partial(per_device, head_devices=mesh.shape["head"]),
        mesh=mesh,
        in_specs=placed,
        out_specs=P(("grp", "row", "rep"), "head"),
        check_vma=False,
    )
```

```python
import functools
import math

import jax
import jax.numpy as jnp
from jax import lax
from jax.experimental import pallas as pl
from jax.experimental.pallas import tpu as pltpu
from jax.sharding import PartitionSpec as P

DH = 128
CHUNK = 256
MM_CHUNK = 1024


def _split(x):
    hi = x.astype(jnp.bfloat16)
    lo = (x - hi.astype(jnp.float32)).astype(jnp.bfloat16)
    return hi, lo


def _mass_kernel(nb_ref, q_ref, k_ref, lim_ref, *refs, chunk_count, score_scale, first, last,
                 pairs_per_kv, block_of):
    if first:
        out_ref, kcat_ref, s_ref, acc_ref, tops_ref = refs
    else:
        acc_in_ref, out_ref, kcat_ref, s_ref, acc_ref, tops_ref = refs
    hp = pl.program_id(0)
    nb = nb_ref[0]
    nfull = nb_ref[1]
    row_count = q_ref.shape[0]
    lanes = 2 * row_count

    @pl.when(hp == 0)
    def _():
        if first:
            acc_ref[...] = jnp.zeros_like(acc_ref)
        else:
            acc_ref[...] = acc_in_ref[...]

    @pl.when(hp % pairs_per_kv == 0)
    def _():
        for c in range(chunk_count):
            @pl.when(block_of[c] < nb)
            def _():
                hi, lo = _split(k_ref[c * CHUNK:(c + 1) * CHUNK, :])
                kcat_ref[c * CHUNK:(c + 1) * CHUNK, :] = jnp.concatenate([hi, hi, lo], axis=1)

    q = q_ref[...]
    xs = []
    for j in range(2):
        qj = q[:, j * DH:(j + 1) * DH]
        xs.append(jnp.concatenate([jnp.maximum(qj, 0.0), jnp.minimum(qj, 0.0)], axis=1).T)
    w = jnp.concatenate(xs, axis=1) * score_scale
    whi, wlo = _split(w)
    wcat = jnp.concatenate([whi, wlo, whi], axis=0)
    lim = lim_ref[...]
    lim2 = jnp.concatenate([lim, lim], axis=1)
    page_in_chunk = lax.broadcasted_iota(jnp.int32, (CHUNK, lanes), 0)

    def vreg_fold(v, op):
        return op(v.reshape(CHUNK // 8, 8, lanes), axis=0)

    mm_pages = min(MM_CHUNK, chunk_count * CHUNK)
    per_mm = mm_pages // CHUNK
    for mc in range(chunk_count * CHUNK // mm_pages):
        @pl.when(min(block_of[mc * per_mm:(mc + 1) * per_mm]) < nb)
        def _():
            s = jnp.dot(kcat_ref[mc * mm_pages:(mc + 1) * mm_pages, :], wcat,
                        preferred_element_type=jnp.float32)
            s_ref[mc * mm_pages:(mc + 1) * mm_pages, :] = s
            for j in range(per_mm):
                c = mc * per_mm + j
                tops_ref[c * 8:(c + 1) * 8, :] = vreg_fold(s[j * CHUNK:(j + 1) * CHUNK, :], jnp.max)

    top = jnp.full((8, lanes), -jnp.inf, jnp.float32)
    for c in range(chunk_count):
        def keep(top):
            return top

        def open_chunk(top, c=c):
            return jnp.maximum(top, tops_ref[c * 8:(c + 1) * 8, :])

        def masked_chunk(top, c=c):
            s = s_ref[c * CHUNK:(c + 1) * CHUNK, :]
            s = jnp.where(page_in_chunk <= lim2 - block_of[c] * CHUNK, s, -1e30)
            s_ref[c * CHUNK:(c + 1) * CHUNK, :] = s
            return jnp.maximum(top, vreg_fold(s, jnp.max))

        branch = jnp.where(block_of[c] < nb, jnp.where(block_of[c] < nfull, 1, 2), 0)
        top = lax.switch(branch, [keep, open_chunk, masked_chunk], top)
    top = jnp.max(top, axis=0, keepdims=True)

    total = jnp.zeros((8, lanes), jnp.float32)
    for c in range(chunk_count):
        def pass_exp(total, c=c):
            e = jnp.exp2(s_ref[c * CHUNK:(c + 1) * CHUNK, :] - top)
            s_ref[c * CHUNK:(c + 1) * CHUNK, :] = e
            return total + vreg_fold(e, jnp.sum)
        total = lax.cond(block_of[c] < nb, pass_exp, lambda t: t, total)
    inv = 1.0 / jnp.sum(total, axis=0, keepdims=True)
    inv_a = inv[:, :row_count]
    inv_b = inv[:, row_count:]

    for c in range(chunk_count):
        @pl.when(block_of[c] < nb)
        def _():
            e = s_ref[c * CHUNK:(c + 1) * CHUNK, :]
            acc_ref[c * CHUNK:(c + 1) * CHUNK, :] += (
                e[:, :row_count] * inv_a + e[:, row_count:] * inv_b)

    @pl.when(hp == pl.num_programs(0) - 1)
    def _():
        for c in range(chunk_count):
            if last:
                out_ref[:, block_of[c] * CHUNK:(block_of[c] + 1) * CHUNK] = acc_ref[c * CHUNK:(c + 1) * CHUNK, :].T
            else:
                out_ref[c * CHUNK:(c + 1) * CHUNK, :] = acc_ref[c * CHUNK:(c + 1) * CHUNK, :]


def page_mass_group(nb, queries, keys, limits, acc, last, block_of):
    row_count = queries.shape[0]
    pair_count = queries.shape[1] // (2 * DH)
    pairs_per_kv = pair_count // (keys.shape[1] // (2 * DH))
    page_count = keys.shape[0]
    chunk_count = page_count // CHUNK
    first = acc is None
    kernel = functools.partial(
        _mass_kernel, chunk_count=chunk_count, score_scale=math.log2(math.e) / math.sqrt(DH),
        first=first, last=last, pairs_per_kv=pairs_per_kv,
        block_of=block_of)
    in_specs = [
        pl.BlockSpec((row_count, 2 * DH), lambda hp, nb: (0, hp)),
        pl.BlockSpec((page_count, 2 * DH), lambda hp, nb: (0, hp // pairs_per_kv)),
        pl.BlockSpec((1, row_count), lambda hp, nb: (0, 0)),
    ]
    operands = [nb, queries, keys, limits.reshape(1, row_count)]
    if not first:
        in_specs.append(pl.BlockSpec((page_count, row_count), lambda hp, nb: (0, 0)))
        operands.append(acc)
    if last:
        out_shape = (row_count, page_count)
    else:
        out_shape = (page_count, row_count)
    aliases = {4: 0} if (not first and not last) else {}
    grid_spec = pltpu.PrefetchScalarGridSpec(
        num_scalar_prefetch=1,
        grid=(pair_count,),
        in_specs=in_specs,
        out_specs=pl.BlockSpec(out_shape, lambda hp, nb: (0, 0)),
        scratch_shapes=[
            pltpu.VMEM((page_count, 6 * DH), jnp.bfloat16),
            pltpu.VMEM((page_count, 2 * row_count), jnp.float32),
            pltpu.VMEM((page_count, row_count), jnp.float32),
            pltpu.VMEM((chunk_count * 8, 2 * row_count), jnp.float32),
        ],
    )
    return pl.pallas_call(
        kernel,
        grid_spec=grid_spec,
        out_shape=jax.ShapeDtypeStruct(out_shape, jnp.float32),
        input_output_aliases=aliases,
        compiler_params=pltpu.CompilerParams(dimension_semantics=("arbitrary",)),
    )(*operands)


def head_sum_scatter(acc, head_devices):
    if head_devices != 2:
        return lax.psum_scatter(acc, "head", scatter_dimension=1, tiled=True)
    half = acc.shape[1] // 2
    first_half = lax.axis_index("head") == 0
    own = jnp.where(first_half, acc[:, :half], acc[:, half:])
    other = jnp.where(first_half, acc[:, half:], acc[:, :half])
    return own + lax.ppermute(other, "head", [(0, 1), (1, 0)])


def per_device(queries, key_max, key_min, limits, head_devices, row_devices, rep_devices):
    local_pages = key_max.shape[0]
    kv_count = key_max.shape[1] // DH
    head_cols = queries.shape[1] // kv_count
    assert local_pages == CHUNK
    block_of = tuple(z * rep_devices + r for r in range(rep_devices) for z in range(row_devices))
    sizes = [kv_count - 1, 1] if kv_count > 1 else [kv_count]
    nb = jnp.stack([jnp.max(limits) // CHUNK + 1, (jnp.min(limits) + 1) // CHUNK]).astype(jnp.int32)
    acc = None
    kv0 = 0
    for g, size in enumerate(sizes):
        parts = []
        for kv in range(kv0, kv0 + size):
            parts += [key_max[:, kv * DH:(kv + 1) * DH], key_min[:, kv * DH:(kv + 1) * DH]]
        keys = lax.all_gather(jnp.concatenate(parts, axis=1), "row", axis=0, tiled=True)
        keys = lax.all_gather(keys, "rep", axis=0, tiled=True)
        cols = slice(kv0 * head_cols, (kv0 + size) * head_cols)
        acc = page_mass_group(nb, queries[:, cols], keys, limits, acc,
                              last=g == len(sizes) - 1, block_of=block_of)
        kv0 += size
    return head_sum_scatter(acc, head_devices)


def solution(mesh):
    placed = (
        P(("grp", "row", "rep"), "head"),
        P(("grp", "row", "rep"), "head"),
        P(("grp", "row", "rep"), "head"),
        P(("grp", "row", "rep")),
    )
    return jax.shard_map(
        functools.partial(per_device, head_devices=mesh.shape["head"], row_devices=mesh.shape["row"],
            rep_devices=mesh.shape["rep"]),
        mesh=mesh,
        in_specs=placed,
        out_specs=P(("grp", "row", "rep"), "head"),
        check_vma=False,
    )
```

```python
import functools
import math

import jax
import jax.numpy as jnp
from jax import lax
from jax.experimental import pallas as pl
from jax.experimental.pallas import tpu as pltpu
from jax.sharding import PartitionSpec as P

DH = 128
CHUNK = 256
MM_CHUNK = 1024


def _split(x):
    hi = x.astype(jnp.bfloat16)
    lo = (x - hi.astype(jnp.float32)).astype(jnp.bfloat16)
    return hi, lo


def _mass_kernel(q_ref, k_ref, lim_ref, *refs, chunk_count, score_scale, first, last,
                 pairs_per_kv, pair_count):
    if first:
        out_ref, kcat_ref, s0_ref, s1_ref, top_ref, acc_ref = refs
    else:
        acc_in_ref, out_ref, kcat_ref, s0_ref, s1_ref, top_ref, acc_ref = refs
    j = pl.program_id(0)
    row_count = q_ref.shape[0]
    lanes = 2 * row_count
    mm_pages = min(MM_CHUNK, chunk_count * CHUNK)
    per_mm = mm_pages // CHUNK

    @pl.when(j == 0)
    def _():
        if first:
            acc_ref[...] = jnp.zeros_like(acc_ref)
        else:
            acc_ref[...] = acc_in_ref[...]

    @pl.when((j < pair_count) & (j % pairs_per_kv == 0))
    def _():
        for c in range(chunk_count):
            hi, lo = _split(k_ref[c * CHUNK:(c + 1) * CHUNK, :])
            kcat_ref[c * CHUNK:(c + 1) * CHUNK, :] = jnp.concatenate([hi, hi, lo], axis=1)

    def vreg_fold(v, op):
        return op(v.reshape(CHUNK // 8, 8, lanes), axis=0)

    def step(new, old):
        top_old = None
        total = jnp.zeros((8, lanes), jnp.float32)
        if old is not None:
            s_old, slot_old = old
            top_old = jnp.max(top_ref[slot_old], axis=0, keepdims=True)
        if new is not None:
            s_new, slot_new = new
            q = q_ref[...]
            xs = []
            for h in range(2):
                qh = q[:, h * DH:(h + 1) * DH]
                xs.append(jnp.concatenate([jnp.maximum(qh, 0.0), jnp.minimum(qh, 0.0)], axis=1).T)
            w = jnp.concatenate(xs, axis=1) * score_scale
            whi, wlo = _split(w)
            wcat = jnp.concatenate([whi, wlo, whi], axis=0)
            lim = lim_ref[...]
            lim2 = jnp.concatenate([lim, lim], axis=1)
            page_in_chunk = lax.broadcasted_iota(jnp.int32, (CHUNK, lanes), 0)
            top = jnp.full((8, lanes), -jnp.inf, jnp.float32)
        for mc in range(chunk_count // per_mm):
            if new is not None:
                s = jnp.dot(kcat_ref[mc * mm_pages:(mc + 1) * mm_pages, :], wcat,
                            preferred_element_type=jnp.float32)
            for i in range(per_mm):
                c = mc * per_mm + i
                if new is not None:
                    sc = jnp.where(page_in_chunk <= lim2 - c * CHUNK,
                                   s[i * CHUNK:(i + 1) * CHUNK, :], -1e30)
                    s_new[c * CHUNK:(c + 1) * CHUNK, :] = sc
                    top = jnp.maximum(top, vreg_fold(sc, jnp.max))
                if old is not None:
                    e = jnp.exp2(s_old[c * CHUNK:(c + 1) * CHUNK, :] - top_old)
                    s_old[c * CHUNK:(c + 1) * CHUNK, :] = e
                    total = total + vreg_fold(e, jnp.sum)
        if new is not None:
            top_ref[slot_new] = top
        if old is not None:
            inv = 1.0 / jnp.sum(total, axis=0, keepdims=True)
            inv_a = inv[:, :row_count]
            inv_b = inv[:, row_count:]
            for c in range(chunk_count):
                e = s_old[c * CHUNK:(c + 1) * CHUNK, :]
                acc_ref[c * CHUNK:(c + 1) * CHUNK, :] += (
                    e[:, :row_count] * inv_a + e[:, row_count:] * inv_b)

    middle = (j >= 1) & (j < pair_count)

    @pl.when(j == 0)
    def _():
        step((s0_ref, 0), None)

    @pl.when(middle & (j % 2 == 1))
    def _():
        step((s1_ref, 1), (s0_ref, 0))

    @pl.when(middle & (j % 2 == 0))
    def _():
        step((s0_ref, 0), (s1_ref, 1))

    @pl.when(j == pair_count)
    def _():
        if (pair_count - 1) % 2 == 0:
            step(None, (s0_ref, 0))
        else:
            step(None, (s1_ref, 1))
        for c in range(chunk_count):
            if last:
                out_ref[:, c * CHUNK:(c + 1) * CHUNK] = acc_ref[c * CHUNK:(c + 1) * CHUNK, :].T
            else:
                out_ref[c * CHUNK:(c + 1) * CHUNK, :] = acc_ref[c * CHUNK:(c + 1) * CHUNK, :]


def page_mass_group(queries, keys, limits, acc, last):
    row_count = queries.shape[0]
    pair_count = queries.shape[1] // (2 * DH)
    pairs_per_kv = pair_count // (keys.shape[1] // (2 * DH))
    page_count = keys.shape[0]
    chunk_count = page_count // CHUNK
    first = acc is None
    kernel = functools.partial(
        _mass_kernel, chunk_count=chunk_count, score_scale=math.log2(math.e) / math.sqrt(DH),
        first=first, last=last, pairs_per_kv=pairs_per_kv, pair_count=pair_count)

    def pair_of(j):
        return jnp.minimum(j, pair_count - 1)

    in_specs = [
        pl.BlockSpec((row_count, 2 * DH), lambda j: (0, pair_of(j))),
        pl.BlockSpec((page_count, 2 * DH), lambda j: (0, pair_of(j) // pairs_per_kv)),
        pl.BlockSpec((1, row_count), lambda j: (0, 0)),
    ]
    operands = [queries, keys, limits.reshape(1, row_count)]
    if not first:
        in_specs.append(pl.BlockSpec((page_count, row_count), lambda j: (0, 0)))
        operands.append(acc)
    if last:
        out_shape = (row_count, page_count)
    else:
        out_shape = (page_count, row_count)
    aliases = {3: 0} if (not first and not last) else {}
    return pl.pallas_call(
        kernel,
        grid=(pair_count + 1,),
        in_specs=in_specs,
        out_specs=pl.BlockSpec(out_shape, lambda j: (0, 0)),
        scratch_shapes=[
            pltpu.VMEM((page_count, 6 * DH), jnp.bfloat16),
            pltpu.VMEM((page_count, 2 * row_count), jnp.float32),
            pltpu.VMEM((page_count, 2 * row_count), jnp.float32),
            pltpu.VMEM((2, 8, 2 * row_count), jnp.float32),
            pltpu.VMEM((page_count, row_count), jnp.float32),
        ],
        out_shape=jax.ShapeDtypeStruct(out_shape, jnp.float32),
        input_output_aliases=aliases,
        compiler_params=pltpu.CompilerParams(dimension_semantics=("arbitrary",)),
    )(*operands)


def head_sum_scatter(acc, head_devices):
    if head_devices != 2:
        return lax.psum_scatter(acc, "head", scatter_dimension=1, tiled=True)
    half = acc.shape[1] // 2
    first_half = lax.axis_index("head") == 0
    own = jnp.where(first_half, acc[:, :half], acc[:, half:])
    other = jnp.where(first_half, acc[:, half:], acc[:, :half])
    return own + lax.ppermute(other, "head", [(0, 1), (1, 0)])


def per_device(queries, key_max, key_min, limits, head_devices):
    local_pages = key_max.shape[0]
    kv_count = key_max.shape[1] // DH
    head_cols = queries.shape[1] // kv_count
    sizes = [kv_count - 1, 1] if kv_count > 1 else [kv_count]
    acc = None
    kv0 = 0
    for g, size in enumerate(sizes):
        parts = []
        for kv in range(kv0, kv0 + size):
            parts += [key_max[:, kv * DH:(kv + 1) * DH], key_min[:, kv * DH:(kv + 1) * DH]]
        keys = lax.all_gather(jnp.concatenate(parts, axis=1), ("row", "rep"), axis=0, tiled=True)
        cols = slice(kv0 * head_cols, (kv0 + size) * head_cols)
        acc = page_mass_group(queries[:, cols], keys, limits, acc, last=g == len(sizes) - 1)
        kv0 += size
    return head_sum_scatter(acc, head_devices)


def solution(mesh):
    placed = (
        P(("grp", "row", "rep"), "head"),
        P(("grp", "row", "rep"), "head"),
        P(("grp", "row", "rep"), "head"),
        P(("grp", "row", "rep")),
    )
    return jax.shard_map(
        functools.partial(per_device, head_devices=mesh.shape["head"]),
        mesh=mesh,
        in_specs=placed,
        out_specs=P(("grp", "row", "rep"), "head"),
        check_vma=False,
    )
```

```python
import functools
import math

import jax
import jax.numpy as jnp
from jax import lax
from jax.experimental import pallas as pl
from jax.experimental.pallas import tpu as pltpu
from jax.sharding import PartitionSpec as P

DH = 128
CHUNK = 256
MM_CHUNK = 1024


def _split(x):
    hi = x.astype(jnp.bfloat16)
    lo = (x - hi.astype(jnp.float32)).astype(jnp.bfloat16)
    return hi, lo


def _mass_kernel(q_ref, k_ref, lim_ref, *refs, chunk_count, score_scale, first, last,
                 pairs_per_kv, pair_count, halves):
    refs = list(refs)
    acc_in_ref = None if first else refs.pop(0)
    out_refs = [refs.pop(0) for _ in range(2 if halves else 1)]
    kcat_ref, s0_ref, s1_ref, top_ref, acc_ref = refs
    out_ref = out_refs[0]
    j = pl.program_id(0)
    row_count = q_ref.shape[0]
    lanes = 2 * row_count
    mm_pages = min(MM_CHUNK, chunk_count * CHUNK)
    per_mm = mm_pages // CHUNK

    @pl.when(j == 0)
    def _():
        if first:
            acc_ref[...] = jnp.zeros_like(acc_ref)
        else:
            acc_ref[...] = acc_in_ref[...]

    @pl.when((j < pair_count) & (j % pairs_per_kv == 0))
    def _():
        for c in range(chunk_count):
            hi, lo = _split(k_ref[c * CHUNK:(c + 1) * CHUNK, :])
            kcat_ref[c * CHUNK:(c + 1) * CHUNK, :] = jnp.concatenate([hi, hi, lo], axis=1)

    def vreg_fold(v, op):
        return op(v.reshape(CHUNK // 8, 8, lanes), axis=0)

    def step(new, old):
        top_old = None
        total = jnp.zeros((8, lanes), jnp.float32)
        if old is not None:
            s_old, slot_old = old
            top_old = jnp.max(top_ref[slot_old], axis=0, keepdims=True)
        if new is not None:
            s_new, slot_new = new
            q = q_ref[...]
            xs = []
            for h in range(2):
                qh = q[:, h * DH:(h + 1) * DH]
                xs.append(jnp.concatenate([jnp.maximum(qh, 0.0), jnp.minimum(qh, 0.0)], axis=1).T)
            w = jnp.concatenate(xs, axis=1) * score_scale
            whi, wlo = _split(w)
            wcat = jnp.concatenate([whi, wlo, whi], axis=0)
            lim = lim_ref[...]
            lim2 = jnp.concatenate([lim, lim], axis=1)
            page_in_chunk = lax.broadcasted_iota(jnp.int32, (CHUNK, lanes), 0)
            top = jnp.full((8, lanes), -jnp.inf, jnp.float32)
        for mc in range(chunk_count // per_mm):
            if new is not None:
                s = jnp.dot(kcat_ref[mc * mm_pages:(mc + 1) * mm_pages, :], wcat,
                            preferred_element_type=jnp.float32)
            for i in range(per_mm):
                c = mc * per_mm + i
                if new is not None:
                    sc = jnp.where(page_in_chunk <= lim2 - c * CHUNK,
                                   s[i * CHUNK:(i + 1) * CHUNK, :], -1e30)
                    s_new[c * CHUNK:(c + 1) * CHUNK, :] = sc
                    top = jnp.maximum(top, vreg_fold(sc, jnp.max))
                if old is not None:
                    e = jnp.exp2(s_old[c * CHUNK:(c + 1) * CHUNK, :] - top_old)
                    s_old[c * CHUNK:(c + 1) * CHUNK, :] = e
                    total = total + vreg_fold(e, jnp.sum)
        if new is not None:
            top_ref[slot_new] = top
        if old is not None:
            inv = 1.0 / jnp.sum(total, axis=0, keepdims=True)
            inv_a = inv[:, :row_count]
            inv_b = inv[:, row_count:]
            for c in range(chunk_count):
                e = s_old[c * CHUNK:(c + 1) * CHUNK, :]
                acc_ref[c * CHUNK:(c + 1) * CHUNK, :] += (
                    e[:, :row_count] * inv_a + e[:, row_count:] * inv_b)

    middle = (j >= 1) & (j < pair_count)

    @pl.when(j == 0)
    def _():
        step((s0_ref, 0), None)

    @pl.when(middle & (j % 2 == 1))
    def _():
        step((s1_ref, 1), (s0_ref, 0))

    @pl.when(middle & (j % 2 == 0))
    def _():
        step((s0_ref, 0), (s1_ref, 1))

    @pl.when(j == pair_count)
    def _():
        if (pair_count - 1) % 2 == 0:
            step(None, (s0_ref, 0))
        else:
            step(None, (s1_ref, 1))
        if halves:
            half = chunk_count // 2
            for own_first in (True, False):
                @pl.when((lax.axis_index("head") == 0) == own_first)
                def _():
                    for c in range(chunk_count):
                        ref = out_refs[0 if (c < half) == own_first else 1]
                        k = c % half
                        ref[:, k * CHUNK:(k + 1) * CHUNK] = acc_ref[c * CHUNK:(c + 1) * CHUNK, :].T
        for c in range(chunk_count if not halves else 0):
            if last:
                out_ref[:, c * CHUNK:(c + 1) * CHUNK] = acc_ref[c * CHUNK:(c + 1) * CHUNK, :].T
            else:
                out_ref[c * CHUNK:(c + 1) * CHUNK, :] = acc_ref[c * CHUNK:(c + 1) * CHUNK, :]


def page_mass_group(queries, keys, limits, acc, last, halves=False):
    row_count = queries.shape[0]
    pair_count = queries.shape[1] // (2 * DH)
    pairs_per_kv = pair_count // (keys.shape[1] // (2 * DH))
    page_count = keys.shape[0]
    chunk_count = page_count // CHUNK
    first = acc is None
    kernel = functools.partial(
        _mass_kernel, chunk_count=chunk_count, score_scale=math.log2(math.e) / math.sqrt(DH),
        first=first, last=last, pairs_per_kv=pairs_per_kv, pair_count=pair_count,
        halves=halves)

    def pair_of(j):
        return jnp.minimum(j, pair_count - 1)

    in_specs = [
        pl.BlockSpec((row_count, 2 * DH), lambda j: (0, pair_of(j))),
        pl.BlockSpec((page_count, 2 * DH), lambda j: (0, pair_of(j) // pairs_per_kv)),
        pl.BlockSpec((1, row_count), lambda j: (0, 0)),
    ]
    operands = [queries, keys, limits.reshape(1, row_count)]
    if not first:
        in_specs.append(pl.BlockSpec((page_count, row_count), lambda j: (0, 0)))
        operands.append(acc)
    if last:
        out_shape = (row_count, page_count)
    else:
        out_shape = (page_count, row_count)
    aliases = {3: 0} if (not first and not last) else {}
    if halves:
        out_shape = (row_count, page_count // 2)
    out_specs = pl.BlockSpec(out_shape, lambda j: (0, 0))
    out_struct = jax.ShapeDtypeStruct(out_shape, jnp.float32)
    if halves:
        out_specs = [out_specs, out_specs]
        out_struct = [out_struct, out_struct]
    return pl.pallas_call(
        kernel,
        grid=(pair_count + 1,),
        in_specs=in_specs,
        out_specs=out_specs,
        scratch_shapes=[
            pltpu.VMEM((page_count, 6 * DH), jnp.bfloat16),
            pltpu.VMEM((page_count, 2 * row_count), jnp.float32),
            pltpu.VMEM((page_count, 2 * row_count), jnp.float32),
            pltpu.VMEM((2, 8, 2 * row_count), jnp.float32),
            pltpu.VMEM((page_count, row_count), jnp.float32),
        ],
        out_shape=out_struct,
        input_output_aliases=aliases,
        compiler_params=pltpu.CompilerParams(dimension_semantics=("arbitrary",)),
    )(*operands)


def head_sum_scatter(acc, head_devices):
    if head_devices != 2:
        return lax.psum_scatter(acc, "head", scatter_dimension=1, tiled=True)
    own, other = acc
    return own + lax.ppermute(other, "head", [(0, 1), (1, 0)])


def per_device(queries, key_max, key_min, limits, head_devices):
    local_pages = key_max.shape[0]
    kv_count = key_max.shape[1] // DH
    head_cols = queries.shape[1] // kv_count
    sizes = [kv_count - 1, 1] if kv_count > 1 else [kv_count]
    acc = None
    kv0 = 0
    for g, size in enumerate(sizes):
        parts = []
        for kv in range(kv0, kv0 + size):
            parts += [key_max[:, kv * DH:(kv + 1) * DH], key_min[:, kv * DH:(kv + 1) * DH]]
        keys = lax.all_gather(jnp.concatenate(parts, axis=1), ("row", "rep"), axis=0, tiled=True)
        cols = slice(kv0 * head_cols, (kv0 + size) * head_cols)
        last = g == len(sizes) - 1
        acc = page_mass_group(queries[:, cols], keys, limits, acc, last=last,
                              halves=last and head_devices == 2)
        kv0 += size
    return head_sum_scatter(acc, head_devices)


def solution(mesh):
    placed = (
        P(("grp", "row", "rep"), "head"),
        P(("grp", "row", "rep"), "head"),
        P(("grp", "row", "rep"), "head"),
        P(("grp", "row", "rep")),
    )
    return jax.shard_map(
        functools.partial(per_device, head_devices=mesh.shape["head"]),
        mesh=mesh,
        in_specs=placed,
        out_specs=P(("grp", "row", "rep"), "head"),
        check_vma=False,
    )
```

```python
import functools
import math

import jax
import jax.numpy as jnp
from jax import lax
from jax.experimental import pallas as pl
from jax.experimental.pallas import tpu as pltpu
from jax.sharding import PartitionSpec as P

DH = 128
CHUNK = 256
MM_CHUNK = 1024


def _split(x):
    hi = x.astype(jnp.bfloat16)
    lo = (x - hi.astype(jnp.float32)).astype(jnp.bfloat16)
    return hi, lo


def _mass_kernel(q_ref, k_ref, lim_ref, *refs, chunk_count, score_scale, first, last,
                 pairs_per_kv, pair_count, halves):
    refs = list(refs)
    acc_in_ref = None if first else refs.pop(0)
    out_refs = [refs.pop(0) for _ in range(2 if halves else 1)]
    kcat_ref, s0_ref, s1_ref, top_ref, acc_ref = refs
    out_ref = out_refs[0]
    j = pl.program_id(0)
    row_count = q_ref.shape[0]
    lanes = 2 * row_count
    mm_pages = min(MM_CHUNK, chunk_count * CHUNK)
    per_mm = mm_pages // CHUNK

    @pl.when(j == 0)
    def _():
        if first:
            acc_ref[...] = jnp.zeros_like(acc_ref)
        else:
            acc_ref[...] = acc_in_ref[...]

    @pl.when((j < pair_count) & (j % pairs_per_kv == 0))
    def _():
        for c in range(chunk_count):
            hi, lo = _split(k_ref[c * CHUNK:(c + 1) * CHUNK, :])
            kcat_ref[c * CHUNK:(c + 1) * CHUNK, :] = jnp.concatenate([hi, hi, lo], axis=1)

    def vreg_fold(v, op):
        return op(v.reshape(CHUNK // 8, 8, lanes), axis=0)

    def step(new, old):
        top_old = None
        total = jnp.zeros((8, lanes), jnp.float32)
        if old is not None:
            s_old, slot_old = old
            top_old = jnp.max(top_ref[slot_old], axis=0, keepdims=True)
        if new is not None:
            s_new, slot_new = new
            q = q_ref[...]
            xs = []
            for h in range(2):
                qh = q[:, h * DH:(h + 1) * DH]
                xs.append(jnp.concatenate([jnp.maximum(qh, 0.0), jnp.minimum(qh, 0.0)], axis=1).T)
            w = jnp.concatenate(xs, axis=1) * score_scale
            whi, wlo = _split(w)
            wcat = jnp.concatenate([whi, wlo, whi], axis=0)
            lim = lim_ref[...]
            lim2 = jnp.concatenate([lim, lim], axis=1)
            page_in_chunk = lax.broadcasted_iota(jnp.int32, (CHUNK, lanes), 0)
            top = jnp.full((8, lanes), -jnp.inf, jnp.float32)
        for mc in range(chunk_count // per_mm):
            if new is not None:
                s = jnp.dot(kcat_ref[mc * mm_pages:(mc + 1) * mm_pages, :], wcat,
                            preferred_element_type=jnp.float32)
            for i in range(per_mm):
                c = mc * per_mm + i
                if new is not None:
                    sc = jnp.where(page_in_chunk <= lim2 - c * CHUNK,
                                   s[i * CHUNK:(i + 1) * CHUNK, :], -1e30)
                    s_new[c * CHUNK:(c + 1) * CHUNK, :] = sc
                    top = jnp.maximum(top, vreg_fold(sc, jnp.max))
                if old is not None:
                    e = jnp.exp2(s_old[c * CHUNK:(c + 1) * CHUNK, :] - top_old)
                    s_old[c * CHUNK:(c + 1) * CHUNK, :] = e
                    total = total + vreg_fold(e, jnp.sum)
        if new is not None:
            top_ref[slot_new] = top
        if old is not None:
            inv = 1.0 / jnp.sum(total, axis=0, keepdims=True)
            inv_a = inv[:, :row_count]
            inv_b = inv[:, row_count:]
            for c in range(chunk_count):
                e = s_old[c * CHUNK:(c + 1) * CHUNK, :]
                acc_ref[c * CHUNK:(c + 1) * CHUNK, :] += (
                    e[:, :row_count] * inv_a + e[:, row_count:] * inv_b)

    middle = (j >= 1) & (j < pair_count)

    @pl.when(j == 0)
    def _():
        step((s0_ref, 0), None)

    @pl.when(middle & (j % 2 == 1))
    def _():
        step((s1_ref, 1), (s0_ref, 0))

    @pl.when(middle & (j % 2 == 0))
    def _():
        step((s0_ref, 0), (s1_ref, 1))

    @pl.when(j == pair_count)
    def _():
        if (pair_count - 1) % 2 == 0:
            step(None, (s0_ref, 0))
        else:
            step(None, (s1_ref, 1))
        if halves:
            half = chunk_count // 2
            for own_first in (True, False):
                @pl.when((lax.axis_index("head") == 0) == own_first)
                def _():
                    for c in range(chunk_count):
                        ref = out_refs[0 if (c < half) == own_first else 1]
                        k = c % half
                        ref[:, k * CHUNK:(k + 1) * CHUNK] = acc_ref[c * CHUNK:(c + 1) * CHUNK, :].T
        for c in range(chunk_count if not halves else 0):
            if last:
                out_ref[:, c * CHUNK:(c + 1) * CHUNK] = acc_ref[c * CHUNK:(c + 1) * CHUNK, :].T
            else:
                out_ref[c * CHUNK:(c + 1) * CHUNK, :] = acc_ref[c * CHUNK:(c + 1) * CHUNK, :]


def page_mass_group(queries, keys, limits, acc, last, halves=False):
    row_count = queries.shape[0]
    pair_count = queries.shape[1] // (2 * DH)
    pairs_per_kv = pair_count // (keys.shape[1] // (2 * DH))
    page_count = keys.shape[0]
    chunk_count = page_count // CHUNK
    first = acc is None
    kernel = functools.partial(
        _mass_kernel, chunk_count=chunk_count, score_scale=math.log2(math.e) / math.sqrt(DH),
        first=first, last=last, pairs_per_kv=pairs_per_kv, pair_count=pair_count,
        halves=halves)

    def pair_of(j):
        return jnp.minimum(j, pair_count - 1)

    in_specs = [
        pl.BlockSpec((row_count, 2 * DH), lambda j: (0, pair_of(j))),
        pl.BlockSpec((page_count, 2 * DH), lambda j: (0, pair_of(j) // pairs_per_kv)),
        pl.BlockSpec((1, row_count), lambda j: (0, 0)),
    ]
    operands = [queries, keys, limits.reshape(1, row_count)]
    if not first:
        in_specs.append(pl.BlockSpec((page_count, row_count), lambda j: (0, 0)))
        operands.append(acc)
    if last:
        out_shape = (row_count, page_count)
    else:
        out_shape = (page_count, row_count)
    aliases = {3: 0} if (not first and not last) else {}
    if halves:
        out_shape = (row_count, page_count // 2)
    out_specs = pl.BlockSpec(out_shape, lambda j: (0, 0))
    out_struct = jax.ShapeDtypeStruct(out_shape, jnp.float32)
    if halves:
        out_specs = [out_specs, out_specs]
        out_struct = [out_struct, out_struct]
    return pl.pallas_call(
        kernel,
        grid=(pair_count + 1,),
        in_specs=in_specs,
        out_specs=out_specs,
        scratch_shapes=[
            pltpu.VMEM((page_count, 6 * DH), jnp.bfloat16),
            pltpu.VMEM((page_count, 2 * row_count), jnp.float32),
            pltpu.VMEM((page_count, 2 * row_count), jnp.float32),
            pltpu.VMEM((2, 8, 2 * row_count), jnp.float32),
            pltpu.VMEM((page_count, row_count), jnp.float32),
        ],
        out_shape=out_struct,
        input_output_aliases=aliases,
        compiler_params=pltpu.CompilerParams(dimension_semantics=("arbitrary",)),
    )(*operands)


def head_sum_scatter(acc, head_devices):
    if head_devices != 2:
        return lax.psum_scatter(acc, "head", scatter_dimension=1, tiled=True)
    own, other = acc
    return own + lax.ppermute(other, "head", [(0, 1), (1, 0)])


def per_device(queries, key_max, key_min, limits, head_devices):
    local_pages = key_max.shape[0]
    kv_count = key_max.shape[1] // DH
    head_cols = queries.shape[1] // kv_count
    sizes = [kv_count - 1, 1] if kv_count > 1 else [kv_count]
    acc = None
    kv0 = 0
    for g, size in enumerate(sizes):
        span = slice(kv0 * DH, (kv0 + size) * DH)
        bounds = jnp.stack(
            (key_max[:, span].reshape(local_pages, size, DH),
             key_min[:, span].reshape(local_pages, size, DH)), axis=2,
        ).reshape(local_pages, size * 2 * DH)
        keys = lax.all_gather(bounds, ("row", "rep"), axis=0, tiled=True)
        cols = slice(kv0 * head_cols, (kv0 + size) * head_cols)
        last = g == len(sizes) - 1
        acc = page_mass_group(queries[:, cols], keys, limits, acc, last=last,
                              halves=last and head_devices == 2)
        kv0 += size
    return head_sum_scatter(acc, head_devices)


def solution(mesh):
    placed = (
        P(("grp", "row", "rep"), "head"),
        P(("grp", "row", "rep"), "head"),
        P(("grp", "row", "rep"), "head"),
        P(("grp", "row", "rep")),
    )
    return jax.shard_map(
        functools.partial(per_device, head_devices=mesh.shape["head"]),
        mesh=mesh,
        in_specs=placed,
        out_specs=P(("grp", "row", "rep"), "head"),
        check_vma=False,
    )
```

```python
import functools
import math

import jax
import jax.numpy as jnp
from jax import lax
from jax.experimental import pallas as pl
from jax.experimental.pallas import tpu as pltpu
from jax.sharding import PartitionSpec as P

DH = 128
CHUNK = 256
MM_CHUNK = 1024


def _split(x):
    hi = x.astype(jnp.bfloat16)
    lo = (x - hi.astype(jnp.float32)).astype(jnp.bfloat16)
    return hi, lo


def _mass_kernel(q_ref, kmax_ref, kmin_ref, lim_ref, *refs, chunk_count, score_scale, first, last,
                 pairs_per_kv, pair_count, halves):
    refs = list(refs)
    acc_in_ref = None if first else refs.pop(0)
    out_refs = [refs.pop(0) for _ in range(2 if halves else 1)]
    kcat_ref, s0_ref, s1_ref, top_ref, acc_ref = refs
    out_ref = out_refs[0]
    j = pl.program_id(0)
    row_count = q_ref.shape[0]
    lanes = 2 * row_count
    mm_pages = min(MM_CHUNK, chunk_count * CHUNK)
    per_mm = mm_pages // CHUNK

    @pl.when(j == 0)
    def _():
        if first:
            acc_ref[...] = jnp.zeros_like(acc_ref)
        else:
            acc_ref[...] = acc_in_ref[...]

    @pl.when((j < pair_count) & (j % pairs_per_kv == 0))
    def _():
        for c in range(chunk_count):
            hmax, lmax = _split(kmax_ref[c * CHUNK:(c + 1) * CHUNK, :])
            hmin, lmin = _split(kmin_ref[c * CHUNK:(c + 1) * CHUNK, :])
            kcat_ref[c * CHUNK:(c + 1) * CHUNK, :] = jnp.concatenate(
                [hmax, hmin, hmax, hmin, lmax, lmin], axis=1)

    def vreg_fold(v, op):
        return op(v.reshape(CHUNK // 8, 8, lanes), axis=0)

    def step(new, old):
        top_old = None
        total = jnp.zeros((8, lanes), jnp.float32)
        if old is not None:
            s_old, slot_old = old
            top_old = jnp.max(top_ref[slot_old], axis=0, keepdims=True)
        if new is not None:
            s_new, slot_new = new
            q = q_ref[...]
            xs = []
            for h in range(2):
                qh = q[:, h * DH:(h + 1) * DH]
                xs.append(jnp.concatenate([jnp.maximum(qh, 0.0), jnp.minimum(qh, 0.0)], axis=1).T)
            w = jnp.concatenate(xs, axis=1) * score_scale
            whi, wlo = _split(w)
            wcat = jnp.concatenate([whi, wlo, whi], axis=0)
            lim = lim_ref[...]
            lim2 = jnp.concatenate([lim, lim], axis=1)
            page_in_chunk = lax.broadcasted_iota(jnp.int32, (CHUNK, lanes), 0)
            top = jnp.full((8, lanes), -jnp.inf, jnp.float32)
        for mc in range(chunk_count // per_mm):
            if new is not None:
                s = jnp.dot(kcat_ref[mc * mm_pages:(mc + 1) * mm_pages, :], wcat,
                            preferred_element_type=jnp.float32)
            for i in range(per_mm):
                c = mc * per_mm + i
                if new is not None:
                    sc = jnp.where(page_in_chunk <= lim2 - c * CHUNK,
                                   s[i * CHUNK:(i + 1) * CHUNK, :], -1e30)
                    s_new[c * CHUNK:(c + 1) * CHUNK, :] = sc
                    top = jnp.maximum(top, vreg_fold(sc, jnp.max))
                if old is not None:
                    e = jnp.exp2(s_old[c * CHUNK:(c + 1) * CHUNK, :] - top_old)
                    s_old[c * CHUNK:(c + 1) * CHUNK, :] = e
                    total = total + vreg_fold(e, jnp.sum)
        if new is not None:
            top_ref[slot_new] = top
        if old is not None:
            inv = 1.0 / jnp.sum(total, axis=0, keepdims=True)
            inv_a = inv[:, :row_count]
            inv_b = inv[:, row_count:]
            for c in range(chunk_count):
                e = s_old[c * CHUNK:(c + 1) * CHUNK, :]
                acc_ref[c * CHUNK:(c + 1) * CHUNK, :] += (
                    e[:, :row_count] * inv_a + e[:, row_count:] * inv_b)

    middle = (j >= 1) & (j < pair_count)

    @pl.when(j == 0)
    def _():
        step((s0_ref, 0), None)

    @pl.when(middle & (j % 2 == 1))
    def _():
        step((s1_ref, 1), (s0_ref, 0))

    @pl.when(middle & (j % 2 == 0))
    def _():
        step((s0_ref, 0), (s1_ref, 1))

    @pl.when(j == pair_count)
    def _():
        if (pair_count - 1) % 2 == 0:
            step(None, (s0_ref, 0))
        else:
            step(None, (s1_ref, 1))
        if halves:
            half = chunk_count // 2
            for own_first in (True, False):
                @pl.when((lax.axis_index("head") == 0) == own_first)
                def _():
                    for c in range(chunk_count):
                        ref = out_refs[0 if (c < half) == own_first else 1]
                        k = c % half
                        ref[:, k * CHUNK:(k + 1) * CHUNK] = acc_ref[c * CHUNK:(c + 1) * CHUNK, :].T
        for c in range(chunk_count if not halves else 0):
            if last:
                out_ref[:, c * CHUNK:(c + 1) * CHUNK] = acc_ref[c * CHUNK:(c + 1) * CHUNK, :].T
            else:
                out_ref[c * CHUNK:(c + 1) * CHUNK, :] = acc_ref[c * CHUNK:(c + 1) * CHUNK, :]


def page_mass_group(queries, kmax, kmin, limits, acc, last, halves=False):
    row_count = queries.shape[0]
    pair_count = queries.shape[1] // (2 * DH)
    kv_in_group = kmax.shape[1] // (2 * DH)
    pairs_per_kv = pair_count // kv_in_group
    page_count = kmax.shape[0]
    chunk_count = page_count // CHUNK
    first = acc is None
    kernel = functools.partial(
        _mass_kernel, chunk_count=chunk_count, score_scale=math.log2(math.e) / math.sqrt(DH),
        first=first, last=last, pairs_per_kv=pairs_per_kv, pair_count=pair_count,
        halves=halves)

    def pair_of(j):
        return jnp.minimum(j, pair_count - 1)

    in_specs = [
        pl.BlockSpec((row_count, 2 * DH), lambda j: (0, pair_of(j))),
        pl.BlockSpec((page_count, DH), lambda j: (0, pair_of(j) // pairs_per_kv)),
        pl.BlockSpec((page_count, DH), lambda j: (0, kv_in_group + pair_of(j) // pairs_per_kv)),
        pl.BlockSpec((1, row_count), lambda j: (0, 0)),
    ]
    operands = [queries, kmax, kmin, limits.reshape(1, row_count)]
    if not first:
        in_specs.append(pl.BlockSpec((page_count, row_count), lambda j: (0, 0)))
        operands.append(acc)
    if last:
        out_shape = (row_count, page_count)
    else:
        out_shape = (page_count, row_count)
    aliases = {4: 0} if (not first and not last) else {}
    if halves:
        out_shape = (row_count, page_count // 2)
    out_specs = pl.BlockSpec(out_shape, lambda j: (0, 0))
    out_struct = jax.ShapeDtypeStruct(out_shape, jnp.float32)
    if halves:
        out_specs = [out_specs, out_specs]
        out_struct = [out_struct, out_struct]
    return pl.pallas_call(
        kernel,
        grid=(pair_count + 1,),
        in_specs=in_specs,
        out_specs=out_specs,
        scratch_shapes=[
            pltpu.VMEM((page_count, 6 * DH), jnp.bfloat16),
            pltpu.VMEM((page_count, 2 * row_count), jnp.float32),
            pltpu.VMEM((page_count, 2 * row_count), jnp.float32),
            pltpu.VMEM((2, 8, 2 * row_count), jnp.float32),
            pltpu.VMEM((page_count, row_count), jnp.float32),
        ],
        out_shape=out_struct,
        input_output_aliases=aliases,
        compiler_params=pltpu.CompilerParams(dimension_semantics=("arbitrary",)),
    )(*operands)


def head_sum_scatter(acc, head_devices):
    if head_devices != 2:
        return lax.psum_scatter(acc, "head", scatter_dimension=1, tiled=True)
    own, other = acc
    return own + lax.ppermute(other, "head", [(0, 1), (1, 0)])


def per_device(queries, key_max, key_min, limits, head_devices):
    local_pages = key_max.shape[0]
    kv_count = key_max.shape[1] // DH
    head_cols = queries.shape[1] // kv_count
    sizes = [kv_count - 1, 1] if kv_count > 1 else [kv_count]
    acc = None
    kv0 = 0
    for g, size in enumerate(sizes):
        span = slice(kv0 * DH, (kv0 + size) * DH)
        keys = lax.all_gather(jnp.concatenate((key_max[:, span], key_min[:, span]), axis=1),
                              ("row", "rep"), axis=0, tiled=True)
        cols = slice(kv0 * head_cols, (kv0 + size) * head_cols)
        last = g == len(sizes) - 1
        acc = page_mass_group(queries[:, cols], keys, keys, limits, acc, last=last,
                              halves=last and head_devices == 2)
        kv0 += size
    return head_sum_scatter(acc, head_devices)


def solution(mesh):
    placed = (
        P(("grp", "row", "rep"), "head"),
        P(("grp", "row", "rep"), "head"),
        P(("grp", "row", "rep"), "head"),
        P(("grp", "row", "rep")),
    )
    return jax.shard_map(
        functools.partial(per_device, head_devices=mesh.shape["head"]),
        mesh=mesh,
        in_specs=placed,
        out_specs=P(("grp", "row", "rep"), "head"),
        check_vma=False,
    )
```

```python
import functools
import math

import jax
import jax.numpy as jnp
from jax import lax
from jax.experimental import pallas as pl
from jax.experimental.pallas import tpu as pltpu
from jax.sharding import PartitionSpec as P

DH = 128
CHUNK = 256
MM_CHUNK = 2048


def _split(x):
    hi = x.astype(jnp.bfloat16)
    lo = (x - hi.astype(jnp.float32)).astype(jnp.bfloat16)
    return hi, lo


def _mass_kernel(q_ref, kmax_ref, kmin_ref, lim_ref, *refs, chunk_count, score_scale, first, last,
                 pairs_per_kv, pair_count, halves):
    refs = list(refs)
    acc_in_ref = None if first else refs.pop(0)
    out_refs = [refs.pop(0) for _ in range(2 if halves else 1)]
    kcat_ref, s0_ref, s1_ref, top_ref, acc_ref = refs
    out_ref = out_refs[0]
    j = pl.program_id(0)
    row_count = q_ref.shape[0]
    lanes = 2 * row_count
    mm_pages = min(MM_CHUNK, chunk_count * CHUNK)
    per_mm = mm_pages // CHUNK

    @pl.when(j == 0)
    def _():
        if first:
            acc_ref[...] = jnp.zeros_like(acc_ref)
        else:
            acc_ref[...] = acc_in_ref[...]

    @pl.when((j < pair_count) & (j % pairs_per_kv == 0))
    def _():
        for c in range(chunk_count):
            hmax, lmax = _split(kmax_ref[c * CHUNK:(c + 1) * CHUNK, :])
            hmin, lmin = _split(kmin_ref[c * CHUNK:(c + 1) * CHUNK, :])
            kcat_ref[c * CHUNK:(c + 1) * CHUNK, :] = jnp.concatenate(
                [hmax, hmin, hmax, hmin, lmax, lmin], axis=1)

    def vreg_fold(v, op):
        return op(v.reshape(CHUNK // 8, 8, lanes), axis=0)

    def step(new, old):
        top_old = None
        total = jnp.zeros((8, lanes), jnp.float32)
        if old is not None:
            s_old, slot_old = old
            top_old = jnp.max(top_ref[slot_old], axis=0, keepdims=True)
        if new is not None:
            s_new, slot_new = new
            q = q_ref[...]
            xs = []
            for h in range(2):
                qh = q[:, h * DH:(h + 1) * DH]
                xs.append(jnp.concatenate([jnp.maximum(qh, 0.0), jnp.minimum(qh, 0.0)], axis=1).T)
            w = jnp.concatenate(xs, axis=1) * score_scale
            whi, wlo = _split(w)
            wcat = jnp.concatenate([whi, wlo, whi], axis=0)
            lim = lim_ref[...]
            lim2 = jnp.concatenate([lim, lim], axis=1)
            page_in_chunk = lax.broadcasted_iota(jnp.int32, (CHUNK, lanes), 0)
            top = jnp.full((8, lanes), -jnp.inf, jnp.float32)
        for mc in range(chunk_count // per_mm):
            if new is not None:
                s = jnp.dot(kcat_ref[mc * mm_pages:(mc + 1) * mm_pages, :], wcat,
                            preferred_element_type=jnp.float32)
            for i in range(per_mm):
                c = mc * per_mm + i
                if new is not None:
                    sc = jnp.where(page_in_chunk <= lim2 - c * CHUNK,
                                   s[i * CHUNK:(i + 1) * CHUNK, :], -1e30)
                    s_new[c * CHUNK:(c + 1) * CHUNK, :] = sc
                    top = jnp.maximum(top, vreg_fold(sc, jnp.max))
                if old is not None:
                    e = jnp.exp2(s_old[c * CHUNK:(c + 1) * CHUNK, :] - top_old)
                    s_old[c * CHUNK:(c + 1) * CHUNK, :] = e
                    total = total + vreg_fold(e, jnp.sum)
        if new is not None:
            top_ref[slot_new] = top
        if old is not None:
            inv = 1.0 / jnp.sum(total, axis=0, keepdims=True)
            inv_a = inv[:, :row_count]
            inv_b = inv[:, row_count:]
            for c in range(chunk_count):
                e = s_old[c * CHUNK:(c + 1) * CHUNK, :]
                acc_ref[c * CHUNK:(c + 1) * CHUNK, :] += (
                    e[:, :row_count] * inv_a + e[:, row_count:] * inv_b)

    middle = (j >= 1) & (j < pair_count)

    @pl.when(j == 0)
    def _():
        step((s0_ref, 0), None)

    @pl.when(middle & (j % 2 == 1))
    def _():
        step((s1_ref, 1), (s0_ref, 0))

    @pl.when(middle & (j % 2 == 0))
    def _():
        step((s0_ref, 0), (s1_ref, 1))

    @pl.when(j == pair_count)
    def _():
        if (pair_count - 1) % 2 == 0:
            step(None, (s0_ref, 0))
        else:
            step(None, (s1_ref, 1))
        if halves:
            half = chunk_count // 2
            for own_first in (True, False):
                @pl.when((lax.axis_index("head") == 0) == own_first)
                def _():
                    for c in range(chunk_count):
                        ref = out_refs[0 if (c < half) == own_first else 1]
                        k = c % half
                        ref[:, k * CHUNK:(k + 1) * CHUNK] = acc_ref[c * CHUNK:(c + 1) * CHUNK, :].T
        for c in range(chunk_count if not halves else 0):
            if last:
                out_ref[:, c * CHUNK:(c + 1) * CHUNK] = acc_ref[c * CHUNK:(c + 1) * CHUNK, :].T
            else:
                out_ref[c * CHUNK:(c + 1) * CHUNK, :] = acc_ref[c * CHUNK:(c + 1) * CHUNK, :]


def page_mass_group(queries, kmax, kmin, limits, acc, last, halves=False):
    row_count = queries.shape[0]
    pair_count = queries.shape[1] // (2 * DH)
    kv_in_group = kmax.shape[1] // (2 * DH)
    pairs_per_kv = pair_count // kv_in_group
    page_count = kmax.shape[0]
    chunk_count = page_count // CHUNK
    first = acc is None
    kernel = functools.partial(
        _mass_kernel, chunk_count=chunk_count, score_scale=math.log2(math.e) / math.sqrt(DH),
        first=first, last=last, pairs_per_kv=pairs_per_kv, pair_count=pair_count,
        halves=halves)

    def pair_of(j):
        return jnp.minimum(j, pair_count - 1)

    in_specs = [
        pl.BlockSpec((row_count, 2 * DH), lambda j: (0, pair_of(j))),
        pl.BlockSpec((page_count, DH), lambda j: (0, pair_of(j) // pairs_per_kv)),
        pl.BlockSpec((page_count, DH), lambda j: (0, kv_in_group + pair_of(j) // pairs_per_kv)),
        pl.BlockSpec((1, row_count), lambda j: (0, 0)),
    ]
    operands = [queries, kmax, kmin, limits.reshape(1, row_count)]
    if not first:
        in_specs.append(pl.BlockSpec((page_count, row_count), lambda j: (0, 0)))
        operands.append(acc)
    if last:
        out_shape = (row_count, page_count)
    else:
        out_shape = (page_count, row_count)
    aliases = {4: 0} if (not first and not last) else {}
    if halves:
        out_shape = (row_count, page_count // 2)
    out_specs = pl.BlockSpec(out_shape, lambda j: (0, 0))
    out_struct = jax.ShapeDtypeStruct(out_shape, jnp.float32)
    if halves:
        out_specs = [out_specs, out_specs]
        out_struct = [out_struct, out_struct]
    return pl.pallas_call(
        kernel,
        grid=(pair_count + 1,),
        in_specs=in_specs,
        out_specs=out_specs,
        scratch_shapes=[
            pltpu.VMEM((page_count, 6 * DH), jnp.bfloat16),
            pltpu.VMEM((page_count, 2 * row_count), jnp.float32),
            pltpu.VMEM((page_count, 2 * row_count), jnp.float32),
            pltpu.VMEM((2, 8, 2 * row_count), jnp.float32),
            pltpu.VMEM((page_count, row_count), jnp.float32),
        ],
        out_shape=out_struct,
        input_output_aliases=aliases,
        compiler_params=pltpu.CompilerParams(dimension_semantics=("arbitrary",)),
    )(*operands)


def head_sum_scatter(acc, head_devices):
    if head_devices != 2:
        return lax.psum_scatter(acc, "head", scatter_dimension=1, tiled=True)
    own, other = acc
    return own + lax.ppermute(other, "head", [(0, 1), (1, 0)])


def per_device(queries, key_max, key_min, limits, head_devices):
    local_pages = key_max.shape[0]
    kv_count = key_max.shape[1] // DH
    head_cols = queries.shape[1] // kv_count
    sizes = [kv_count - 1, 1] if kv_count > 1 else [kv_count]
    acc = None
    kv0 = 0
    for g, size in enumerate(sizes):
        span = slice(kv0 * DH, (kv0 + size) * DH)
        keys = lax.all_gather(jnp.concatenate((key_max[:, span], key_min[:, span]), axis=1),
                              ("row", "rep"), axis=0, tiled=True)
        cols = slice(kv0 * head_cols, (kv0 + size) * head_cols)
        last = g == len(sizes) - 1
        acc = page_mass_group(queries[:, cols], keys, keys, limits, acc, last=last,
                              halves=last and head_devices == 2)
        kv0 += size
    return head_sum_scatter(acc, head_devices)


def solution(mesh):
    placed = (
        P(("grp", "row", "rep"), "head"),
        P(("grp", "row", "rep"), "head"),
        P(("grp", "row", "rep"), "head"),
        P(("grp", "row", "rep")),
    )
    return jax.shard_map(
        functools.partial(per_device, head_devices=mesh.shape["head"]),
        mesh=mesh,
        in_specs=placed,
        out_specs=P(("grp", "row", "rep"), "head"),
        check_vma=False,
    )
```

```python
import functools
import math

import jax
import jax.numpy as jnp
from jax import lax
from jax.experimental import pallas as pl
from jax.experimental.pallas import tpu as pltpu
from jax.sharding import PartitionSpec as P

DH = 128
CHUNK = 256
MM_CHUNK = 1024


def _split(x):
    hi = x.astype(jnp.bfloat16)
    lo = (x - hi.astype(jnp.float32)).astype(jnp.bfloat16)
    return hi, lo


def _mass_kernel(q_ref, kmax_ref, kmin_ref, lim_ref, *refs, chunk_count, score_scale, first, last,
                 pairs_per_kv, pair_count, halves):
    refs = list(refs)
    acc_in_ref = None if first else refs.pop(0)
    out_refs = [refs.pop(0) for _ in range(2 if halves else 1)]
    kcat_ref, s0_ref, s1_ref, top_ref, acc_ref = refs
    out_ref = out_refs[0]
    j = pl.program_id(0)
    row_count = q_ref.shape[0]
    lanes = 2 * row_count
    mm_pages = min(MM_CHUNK, chunk_count * CHUNK)
    per_mm = mm_pages // CHUNK

    @pl.when(j == 0)
    def _():
        if first:
            acc_ref[...] = jnp.zeros_like(acc_ref)
        else:
            acc_ref[...] = acc_in_ref[...]

    @pl.when((j < pair_count) & (j % pairs_per_kv == 0))
    def _():
        for c in range(chunk_count):
            hmax, lmax = _split(kmax_ref[c * CHUNK:(c + 1) * CHUNK, :])
            hmin, lmin = _split(kmin_ref[c * CHUNK:(c + 1) * CHUNK, :])
            kcat_ref[c * CHUNK:(c + 1) * CHUNK, :] = jnp.concatenate(
                [hmax, hmin, hmax, hmin, lmax, lmin], axis=1)

    def vreg_fold(v, op):
        return op(v.reshape(CHUNK // 8, 8, lanes), axis=0)

    def step(new, old):
        top_old = None
        total = jnp.zeros((8, lanes), jnp.float32)
        if old is not None:
            s_old, slot_old = old
            top_old = jnp.max(top_ref[slot_old], axis=0, keepdims=True)
        if new is not None:
            s_new, slot_new = new
            q = q_ref[...]
            xs = []
            for h in range(2):
                qh = q[:, h * DH:(h + 1) * DH]
                xs.append(jnp.concatenate([jnp.maximum(qh, 0.0), jnp.minimum(qh, 0.0)], axis=1).T)
            w = jnp.concatenate(xs, axis=1) * score_scale
            whi, wlo = _split(w)
            wcat = jnp.concatenate([whi, wlo, whi], axis=0)
            lim = lim_ref[...]
            lim2 = jnp.concatenate([lim, lim], axis=1)
            page_in_chunk = lax.broadcasted_iota(jnp.int32, (CHUNK, lanes), 0)
            top = jnp.full((8, lanes), -jnp.inf, jnp.float32)
        for mc in range(chunk_count // per_mm):
            if new is not None:
                s = jnp.dot(kcat_ref[mc * mm_pages:(mc + 1) * mm_pages, :], wcat,
                            preferred_element_type=jnp.float32)
            for i in range(per_mm):
                c = mc * per_mm + i
                if new is not None:
                    sc = jnp.where(page_in_chunk <= lim2 - c * CHUNK,
                                   s[i * CHUNK:(i + 1) * CHUNK, :], -1e30)
                    s_new[c * CHUNK:(c + 1) * CHUNK, :] = sc
                    top = jnp.maximum(top, vreg_fold(sc, jnp.max))
                if old is not None:
                    e = jnp.exp2(s_old[c * CHUNK:(c + 1) * CHUNK, :] - top_old)
                    s_old[c * CHUNK:(c + 1) * CHUNK, :] = e
                    total = total + vreg_fold(e, jnp.sum)
        if new is not None:
            top_ref[slot_new] = top
        if old is not None:
            inv = 1.0 / jnp.sum(total, axis=0, keepdims=True)
            inv_a = inv[:, :row_count]
            inv_b = inv[:, row_count:]
            for c in range(chunk_count):
                e = s_old[c * CHUNK:(c + 1) * CHUNK, :]
                acc_ref[c * CHUNK:(c + 1) * CHUNK, :] += (
                    e[:, :row_count] * inv_a + e[:, row_count:] * inv_b)

    middle = (j >= 1) & (j < pair_count)

    @pl.when(j == 0)
    def _():
        step((s0_ref, 0), None)

    @pl.when(middle & (j % 2 == 1))
    def _():
        step((s1_ref, 1), (s0_ref, 0))

    @pl.when(middle & (j % 2 == 0))
    def _():
        step((s0_ref, 0), (s1_ref, 1))

    @pl.when(j == pair_count)
    def _():
        if (pair_count - 1) % 2 == 0:
            step(None, (s0_ref, 0))
        else:
            step(None, (s1_ref, 1))
        if halves:
            half = chunk_count // 2
            for own_first in (True, False):
                @pl.when((lax.axis_index("head") == 0) == own_first)
                def _():
                    for c in range(chunk_count):
                        ref = out_refs[0 if (c < half) == own_first else 1]
                        k = c % half
                        ref[:, k * CHUNK:(k + 1) * CHUNK] = acc_ref[c * CHUNK:(c + 1) * CHUNK, :].T
        for c in range(chunk_count if not halves else 0):
            if last:
                out_ref[:, c * CHUNK:(c + 1) * CHUNK] = acc_ref[c * CHUNK:(c + 1) * CHUNK, :].T
            else:
                out_ref[c * CHUNK:(c + 1) * CHUNK, :] = acc_ref[c * CHUNK:(c + 1) * CHUNK, :]


def page_mass_group(queries, kmax, kmin, limits, acc, last, halves=False):
    row_count = queries.shape[0]
    pair_count = queries.shape[1] // (2 * DH)
    kv_in_group = kmax.shape[2] // DH
    pairs_per_kv = pair_count // kv_in_group
    page_count = kmax.shape[1]
    chunk_count = page_count // CHUNK
    first = acc is None
    kernel = functools.partial(
        _mass_kernel, chunk_count=chunk_count, score_scale=math.log2(math.e) / math.sqrt(DH),
        first=first, last=last, pairs_per_kv=pairs_per_kv, pair_count=pair_count,
        halves=halves)

    def pair_of(j):
        return jnp.minimum(j, pair_count - 1)

    in_specs = [
        pl.BlockSpec((row_count, 2 * DH), lambda j: (0, pair_of(j))),
        pl.BlockSpec((None, page_count, DH), lambda j: (0, 0, pair_of(j) // pairs_per_kv)),
        pl.BlockSpec((None, page_count, DH), lambda j: (1, 0, pair_of(j) // pairs_per_kv)),
        pl.BlockSpec((1, row_count), lambda j: (0, 0)),
    ]
    operands = [queries, kmax, kmin, limits.reshape(1, row_count)]
    if not first:
        in_specs.append(pl.BlockSpec((page_count, row_count), lambda j: (0, 0)))
        operands.append(acc)
    if last:
        out_shape = (row_count, page_count)
    else:
        out_shape = (page_count, row_count)
    aliases = {4: 0} if (not first and not last) else {}
    if halves:
        out_shape = (row_count, page_count // 2)
    out_specs = pl.BlockSpec(out_shape, lambda j: (0, 0))
    out_struct = jax.ShapeDtypeStruct(out_shape, jnp.float32)
    if halves:
        out_specs = [out_specs, out_specs]
        out_struct = [out_struct, out_struct]
    return pl.pallas_call(
        kernel,
        grid=(pair_count + 1,),
        in_specs=in_specs,
        out_specs=out_specs,
        scratch_shapes=[
            pltpu.VMEM((page_count, 6 * DH), jnp.bfloat16),
            pltpu.VMEM((page_count, 2 * row_count), jnp.float32),
            pltpu.VMEM((page_count, 2 * row_count), jnp.float32),
            pltpu.VMEM((2, 8, 2 * row_count), jnp.float32),
            pltpu.VMEM((page_count, row_count), jnp.float32),
        ],
        out_shape=out_struct,
        input_output_aliases=aliases,
        compiler_params=pltpu.CompilerParams(dimension_semantics=("arbitrary",)),
    )(*operands)


def head_sum_scatter(acc, head_devices):
    if head_devices != 2:
        return lax.psum_scatter(acc, "head", scatter_dimension=1, tiled=True)
    own, other = acc
    return own + lax.ppermute(other, "head", [(0, 1), (1, 0)])


def per_device(queries, key_max, key_min, limits, head_devices):
    local_pages = key_max.shape[0]
    kv_count = key_max.shape[1] // DH
    head_cols = queries.shape[1] // kv_count
    sizes = [kv_count - 1, 1] if kv_count > 1 else [kv_count]
    acc = None
    kv0 = 0
    for g, size in enumerate(sizes):
        span = slice(kv0 * DH, (kv0 + size) * DH)
        keys = lax.all_gather(jnp.stack((key_max[:, span], key_min[:, span])),
                              ("row", "rep"), axis=1, tiled=True)
        cols = slice(kv0 * head_cols, (kv0 + size) * head_cols)
        last = g == len(sizes) - 1
        acc = page_mass_group(queries[:, cols], keys, keys, limits, acc, last=last,
                              halves=last and head_devices == 2)
        kv0 += size
    return head_sum_scatter(acc, head_devices)


def solution(mesh):
    placed = (
        P(("grp", "row", "rep"), "head"),
        P(("grp", "row", "rep"), "head"),
        P(("grp", "row", "rep"), "head"),
        P(("grp", "row", "rep")),
    )
    return jax.shard_map(
        functools.partial(per_device, head_devices=mesh.shape["head"]),
        mesh=mesh,
        in_specs=placed,
        out_specs=P(("grp", "row", "rep"), "head"),
        check_vma=False,
    )
```

```python
import functools
import math

import jax
import jax.numpy as jnp
from jax import lax
from jax.experimental import pallas as pl
from jax.experimental.pallas import tpu as pltpu
from jax.sharding import PartitionSpec as P

DH = 128
CHUNK = 256
MM_CHUNK = 512


def _split(x):
    hi = x.astype(jnp.bfloat16)
    lo = (x - hi.astype(jnp.float32)).astype(jnp.bfloat16)
    return hi, lo


def _mass_kernel(q_ref, kmax_ref, kmin_ref, lim_ref, *refs, chunk_count, score_scale, first, last,
                 pairs_per_kv, pair_count, halves):
    refs = list(refs)
    acc_in_ref = None if first else refs.pop(0)
    out_refs = [refs.pop(0) for _ in range(2 if halves else 1)]
    kcat_ref, s0_ref, s1_ref, top_ref, acc_ref = refs
    out_ref = out_refs[0]
    j = pl.program_id(0)
    row_count = q_ref.shape[0]
    lanes = 2 * row_count
    mm_pages = min(MM_CHUNK, chunk_count * CHUNK)
    per_mm = mm_pages // CHUNK

    @pl.when(j == 0)
    def _():
        if first:
            acc_ref[...] = jnp.zeros_like(acc_ref)
        else:
            acc_ref[...] = acc_in_ref[...]

    @pl.when((j < pair_count) & (j % pairs_per_kv == 0))
    def _():
        for c in range(chunk_count):
            hmax, lmax = _split(kmax_ref[c * CHUNK:(c + 1) * CHUNK, :])
            hmin, lmin = _split(kmin_ref[c * CHUNK:(c + 1) * CHUNK, :])
            kcat_ref[c * CHUNK:(c + 1) * CHUNK, :] = jnp.concatenate(
                [hmax, hmin, hmax, hmin, lmax, lmin], axis=1)

    def vreg_fold(v, op):
        return op(v.reshape(CHUNK // 8, 8, lanes), axis=0)

    def step(new, old):
        top_old = None
        total = jnp.zeros((8, lanes), jnp.float32)
        if old is not None:
            s_old, slot_old = old
            top_old = jnp.max(top_ref[slot_old], axis=0, keepdims=True)
        if new is not None:
            s_new, slot_new = new
            q = q_ref[...]
            xs = []
            for h in range(2):
                qh = q[:, h * DH:(h + 1) * DH]
                xs.append(jnp.concatenate([jnp.maximum(qh, 0.0), jnp.minimum(qh, 0.0)], axis=1).T)
            w = jnp.concatenate(xs, axis=1) * score_scale
            whi, wlo = _split(w)
            wcat = jnp.concatenate([whi, wlo, whi], axis=0)
            lim = lim_ref[...]
            lim2 = jnp.concatenate([lim, lim], axis=1)
            page_in_chunk = lax.broadcasted_iota(jnp.int32, (CHUNK, lanes), 0)
            top = jnp.full((8, lanes), -jnp.inf, jnp.float32)
        for mc in range(chunk_count // per_mm):
            if new is not None:
                s = jnp.dot(kcat_ref[mc * mm_pages:(mc + 1) * mm_pages, :], wcat,
                            preferred_element_type=jnp.float32)
            for i in range(per_mm):
                c = mc * per_mm + i
                if new is not None:
                    sc = jnp.where(page_in_chunk <= lim2 - c * CHUNK,
                                   s[i * CHUNK:(i + 1) * CHUNK, :], -1e30)
                    s_new[c * CHUNK:(c + 1) * CHUNK, :] = sc
                    top = jnp.maximum(top, vreg_fold(sc, jnp.max))
                if old is not None:
                    e = jnp.exp2(s_old[c * CHUNK:(c + 1) * CHUNK, :] - top_old)
                    s_old[c * CHUNK:(c + 1) * CHUNK, :] = e
                    total = total + vreg_fold(e, jnp.sum)
        if new is not None:
            top_ref[slot_new] = top
        if old is not None:
            inv = 1.0 / jnp.sum(total, axis=0, keepdims=True)
            inv_a = inv[:, :row_count]
            inv_b = inv[:, row_count:]
            for c in range(chunk_count):
                e = s_old[c * CHUNK:(c + 1) * CHUNK, :]
                acc_ref[c * CHUNK:(c + 1) * CHUNK, :] += (
                    e[:, :row_count] * inv_a + e[:, row_count:] * inv_b)

    middle = (j >= 1) & (j < pair_count)

    @pl.when(j == 0)
    def _():
        step((s0_ref, 0), None)

    @pl.when(middle & (j % 2 == 1))
    def _():
        step((s1_ref, 1), (s0_ref, 0))

    @pl.when(middle & (j % 2 == 0))
    def _():
        step((s0_ref, 0), (s1_ref, 1))

    @pl.when(j == pair_count)
    def _():
        if (pair_count - 1) % 2 == 0:
            step(None, (s0_ref, 0))
        else:
            step(None, (s1_ref, 1))
        if halves:
            half = chunk_count // 2
            for own_first in (True, False):
                @pl.when((lax.axis_index("head") == 0) == own_first)
                def _():
                    for c in range(chunk_count):
                        ref = out_refs[0 if (c < half) == own_first else 1]
                        k = c % half
                        ref[:, k * CHUNK:(k + 1) * CHUNK] = acc_ref[c * CHUNK:(c + 1) * CHUNK, :].T
        for c in range(chunk_count if not halves else 0):
            if last:
                out_ref[:, c * CHUNK:(c + 1) * CHUNK] = acc_ref[c * CHUNK:(c + 1) * CHUNK, :].T
            else:
                out_ref[c * CHUNK:(c + 1) * CHUNK, :] = acc_ref[c * CHUNK:(c + 1) * CHUNK, :]


def page_mass_group(queries, kmax, kmin, limits, acc, last, halves=False):
    row_count = queries.shape[0]
    pair_count = queries.shape[1] // (2 * DH)
    kv_in_group = kmax.shape[2] // DH
    pairs_per_kv = pair_count // kv_in_group
    page_count = kmax.shape[1]
    chunk_count = page_count // CHUNK
    first = acc is None
    kernel = functools.partial(
        _mass_kernel, chunk_count=chunk_count, score_scale=math.log2(math.e) / math.sqrt(DH),
        first=first, last=last, pairs_per_kv=pairs_per_kv, pair_count=pair_count,
        halves=halves)

    def pair_of(j):
        return jnp.minimum(j, pair_count - 1)

    in_specs = [
        pl.BlockSpec((row_count, 2 * DH), lambda j: (0, pair_of(j))),
        pl.BlockSpec((None, page_count, DH), lambda j: (0, 0, pair_of(j) // pairs_per_kv)),
        pl.BlockSpec((None, page_count, DH), lambda j: (1, 0, pair_of(j) // pairs_per_kv)),
        pl.BlockSpec((1, row_count), lambda j: (0, 0)),
    ]
    operands = [queries, kmax, kmin, limits.reshape(1, row_count)]
    if not first:
        in_specs.append(pl.BlockSpec((page_count, row_count), lambda j: (0, 0)))
        operands.append(acc)
    if last:
        out_shape = (row_count, page_count)
    else:
        out_shape = (page_count, row_count)
    aliases = {4: 0} if (not first and not last) else {}
    if halves:
        out_shape = (row_count, page_count // 2)
    out_specs = pl.BlockSpec(out_shape, lambda j: (0, 0))
    out_struct = jax.ShapeDtypeStruct(out_shape, jnp.float32)
    if halves:
        out_specs = [out_specs, out_specs]
        out_struct = [out_struct, out_struct]
    return pl.pallas_call(
        kernel,
        grid=(pair_count + 1,),
        in_specs=in_specs,
        out_specs=out_specs,
        scratch_shapes=[
            pltpu.VMEM((page_count, 6 * DH), jnp.bfloat16),
            pltpu.VMEM((page_count, 2 * row_count), jnp.float32),
            pltpu.VMEM((page_count, 2 * row_count), jnp.float32),
            pltpu.VMEM((2, 8, 2 * row_count), jnp.float32),
            pltpu.VMEM((page_count, row_count), jnp.float32),
        ],
        out_shape=out_struct,
        input_output_aliases=aliases,
        compiler_params=pltpu.CompilerParams(dimension_semantics=("arbitrary",)),
    )(*operands)


def head_sum_scatter(acc, head_devices):
    if head_devices != 2:
        return lax.psum_scatter(acc, "head", scatter_dimension=1, tiled=True)
    own, other = acc
    return own + lax.ppermute(other, "head", [(0, 1), (1, 0)])


def per_device(queries, key_max, key_min, limits, head_devices):
    local_pages = key_max.shape[0]
    kv_count = key_max.shape[1] // DH
    head_cols = queries.shape[1] // kv_count
    sizes = [kv_count - 1, 1] if kv_count > 1 else [kv_count]
    acc = None
    kv0 = 0
    for g, size in enumerate(sizes):
        span = slice(kv0 * DH, (kv0 + size) * DH)
        keys = lax.all_gather(jnp.stack((key_max[:, span], key_min[:, span])),
                              ("row", "rep"), axis=1, tiled=True)
        cols = slice(kv0 * head_cols, (kv0 + size) * head_cols)
        last = g == len(sizes) - 1
        acc = page_mass_group(queries[:, cols], keys, keys, limits, acc, last=last,
                              halves=last and head_devices == 2)
        kv0 += size
    return head_sum_scatter(acc, head_devices)


def solution(mesh):
    placed = (
        P(("grp", "row", "rep"), "head"),
        P(("grp", "row", "rep"), "head"),
        P(("grp", "row", "rep"), "head"),
        P(("grp", "row", "rep")),
    )
    return jax.shard_map(
        functools.partial(per_device, head_devices=mesh.shape["head"]),
        mesh=mesh,
        in_specs=placed,
        out_specs=P(("grp", "row", "rep"), "head"),
        check_vma=False,
    )
```
